32 devices in a mesh: section: 2 (over x), dp: 4 (over z), expert: 4 (over y, core).
Axes of the slice: x: 2, y: 2, z: 4, core: 2. Of those that a mesh axis runs over, the one named last changes fastest.
Arguments:
- grad_out: bfloat16 [2, 2048, 2048], P('section', ('dp', 'expert')), may hold values from -6 to 6
- routes: int32 [2, 2048, 2], P('section', ('dp', 'expert')), may hold values from 0 to 3, all different within a row; in each aligned block of 128 rows (0 to 127, 128 to 255, ..., all dimensions but the last counted through in order) at most 80 rows name the same one
- gates: float32 [2, 2048, 2], P('section', ('dp', 'expert')), may hold values from 0.2 to 1
- hidden: bfloat16 [2, 4, 4, 320, 1408], P('section', 'dp', 'expert'), may hold values from -0.09375 to 0.09375
- w_down: bfloat16 [2, 4, 1408, 2048], P('section', 'expert'), may hold values from -0.15625 to 0.15625
Outputs:
- grad_hidden: bfloat16 [2, 4, 4, 320, 1408], P('section', 'dp', 'expert')
- grad_w_down: float32 [2, 4, 1408, 2048], P('section', 'expert', 'dp')
The draws below stay inside these ranges and needn't reach their ends.
Inputs may be any that keep to these rules, and one draw needn't show every extreme that they name: `routes`: each token names 2 different experts; among the 128 tokens of one device no expert is named more than 80 times, a bound that some block reaches.
All inputs are finite; a program needn't handle non-finite values.
Results may differ from the reference program's by a relative error of at most 0.015.
Values may be sent and summed in bfloat16 or wider, within the bound.
No kernel may reach another device: no remote copies, remote signals or barrier semaphores. Data moves between devices by JAX's collectives and lax.ppermute only.
A program may use at most 64 MiB of HBM per device.

```python
import math
import jax
import jax.numpy as jnp
import numpy as np
from jax import lax

D = 2048
H = 1408
TOPK = 2
TOK_DEV = 128
EXPERTS = 4
CAP = 80
SLOTS = 320
TOKENS = 2048
N_SECTION = 2
N_DP = 4
N_EXPERT = 4


def with_spikes(array, stream_key, source, target, blocks, factor):
    def block_of(dim):
        return (jnp.arange(array.shape[dim]) // (array.shape[dim] // blocks)).reshape((-1,) + (1,) * (array.ndim - 1 - dim))

    near = jax.random.permutation(stream_key, blocks)[block_of(target)]
    second = (block_of(target) + blocks // 2) % blocks
    return jnp.where((block_of(source) == near) | (block_of(source) == second), factor * array, array)


def block_levels(own_key, dims, split, low, top_value):
    factor_of, own = 1.0, jax.random.fold_in(own_key, 6)
    for axis_at, blocks in split:
        steps = jnp.exp(jax.random.uniform(jax.random.fold_in(own, axis_at), (blocks,), jnp.float32, low / len(split), top_value / len(split)))
        factor_of = factor_of * jnp.repeat(steps, dims[axis_at] // blocks).reshape([-1 if axis == axis_at else 1 for axis in range(len(dims))])
    return factor_of


def assign_block(key, own, number, rows, count, top, reach, lean):
    ranking = jax.random.permutation(key, count)
    crowded, common = shares(count, rows * top, reach, lean, True), shares(count, rows * top, reach, lean, False)
    places = jnp.arange(count)

    def named(tallies, turn):
        used = int((tallies > 0).sum())
        fixed = max(1, used // 4)
        moved = fixed + (places - fixed + turn * (used - fixed)) % max(1, count - fixed)
        return jnp.zeros((count,), jnp.int32).at[ranking[jnp.where(places < fixed, places, moved)]].set(jnp.asarray(tallies, jnp.int32))

    tallies = jnp.where(number % 4 == 0, named(crowded, number // 4), named(common, number - number // 4 - 1))
    mixed = jax.random.permutation(jax.random.fold_in(own, 3), count)
    donor, taker = mixed[0:count // 2 * 2:2], mixed[1:count // 2 * 2:2]
    margin = jnp.minimum(tallies[donor] - 1, reach - tallies[taker]) // 2
    margin = jnp.where((donor == ranking[0]) | (taker == ranking[0]) | (tallies[taker] == 0), 0, jnp.maximum(margin, 0))
    moved = jax.random.randint(jax.random.fold_in(own, 4), (count // 2,), 0, 1 << 20) % (margin + 1)
    tallies = tallies.at[donor].add(-moved).at[taker].add(moved)
    members = jnp.searchsorted(jnp.cumsum(tallies), jnp.arange(rows * top), side="right").astype(jnp.int32)
    grid = members.reshape(top, rows).T
    grid = grid[jax.random.permutation(jax.random.fold_in(own, 1), rows)]
    turn = jax.random.randint(jax.random.fold_in(own, 2), (rows, 1), 0, top)
    return jnp.take_along_axis(grid, (jnp.arange(top)[None, :] + turn) % top, axis=1)


def shares(amount, total, bound, skew, full):
    portions = [(1 << 20) // math.isqrt(rank ** skew) + 1 for rank in range(1, amount + 1)]
    largest = bound if full else min(bound, max(-(-total // amount), total * portions[0] // sum(portions)))
    least = 1 if total - largest >= amount - 1 else 0
    given, rest = [largest] + [least] * (amount - 1), total - largest - least * (amount - 1)
    while rest > 0:
        candidates = [i for i in range(1, amount) if given[i] < largest] or [i for i in range(1, amount) if given[i] < bound]
        whole, budget = sum([portions[i] for i in candidates]), rest
        for i in candidates:
            addition = min(bound - given[i], max(1, budget * portions[i] // whole), rest)
            given[i] = given[i] + addition
            rest = rest - addition
    return np.array(given)


def noise(key, shape, spread, reach, cuts=(), held_as=jnp.bfloat16):
    array = spread * jax.random.normal(key, shape, jnp.float32)
    if cuts:
        array = array * block_levels(key, shape, cuts, -0.22, 0.18)
    return jnp.clip(array, -reach, reach).astype(held_as)


def noise_with(rng, dims, spread, reach, shards, heavy, kind=jnp.bfloat16):
    drawn = spread * jax.random.normal(rng, dims, jnp.float32)
    if shards:
        drawn = drawn * block_levels(rng, dims, shards, -0.22, 0.18)
    return jnp.clip(with_spikes(drawn, jax.random.fold_in(rng, 3), *heavy), -reach, reach).astype(kind)


def setup_inputs(seed: int = 0) -> dict:
    streams_of = jax.random.split(jax.random.key(seed), 6)
    grad_out = noise(streams_of[0], (N_SECTION, TOKENS, D), 1.0, 6.0, ((0, 2), (1, 16)))
    routes_keys = jax.random.split(jax.random.fold_in(streams_of[1], 1), N_SECTION * TOKENS // TOK_DEV)
    routes_turns = jax.random.permutation(jax.random.fold_in(streams_of[1], 3), N_SECTION * TOKENS // TOK_DEV)
    routes = jax.vmap(lambda own, number: assign_block(jax.random.fold_in(streams_of[1], 2), own, number, TOK_DEV, EXPERTS, TOPK, CAP, 2))(routes_keys, routes_turns).reshape((N_SECTION, TOKENS, TOPK))
    gates = jnp.clip(0.2 + 0.8 * jax.random.uniform(streams_of[2], (N_SECTION, TOKENS, TOPK), jnp.float32) ** block_levels(streams_of[2], (N_SECTION, TOKENS, TOPK), ((0, 2), (1, 16)), -0.2, 0.2), 0.2, 1.0)
    hidden = noise_with(streams_of[3], (N_SECTION, N_DP, EXPERTS, SLOTS, H), 0.015625, 0.09375, ((0, 2), (1, 4), (2, 4)), (1, 4, 4, 2.0))
    w_down = noise(streams_of[4], (N_SECTION, EXPERTS, H, D), H ** -0.5, 0.15625, ((0, 2), (1, 4)))
    return {"grad_out": grad_out, "routes": routes, "gates": gates, "hidden": hidden, "w_down": w_down}


def dispatch_block(rows, ids, weights, count, width):
    flat_ids = ids.reshape(-1).astype(jnp.int32)
    onehot = (flat_ids[:, None] == jnp.arange(count, dtype=jnp.int32)[None, :]).astype(jnp.int32)
    position = jnp.sum((jnp.cumsum(onehot, axis=0) - 1) * onehot, axis=1).astype(jnp.int32)
    target = flat_ids * width + position
    scaled = (weights[:, :, None].astype(jnp.float32) * rows[:, None, :].astype(jnp.float32)).astype(jnp.bfloat16)
    scaled = scaled.reshape(-1, rows.shape[1])
    buffer = jnp.zeros((count * width, rows.shape[1]), jnp.bfloat16).at[target].set(scaled)
    return buffer.reshape(count, width, rows.shape[1])


def reference(grad_out, routes, gates, hidden, w_down):
    incoming = jnp.roll(grad_out, -1, axis=0)
    hidden_grads = []
    weight_grads = []
    for section_id in range(N_SECTION):
        rows = incoming[section_id].reshape(N_DP * N_EXPERT, TOK_DEV, D)
        ids = routes[section_id].reshape(N_DP * N_EXPERT, TOK_DEV, TOPK)
        weights = gates[section_id].reshape(N_DP * N_EXPERT, TOK_DEV, TOPK)
        sent = jax.vmap(lambda r, i, w: dispatch_block(r, i, w, EXPERTS, CAP))(rows, ids, weights)
        sent = sent.reshape(N_DP, N_EXPERT, EXPERTS, CAP, D)
        scaled = sent.transpose(2, 0, 1, 3, 4).reshape(EXPERTS, N_DP, SLOTS, D)
        saved = hidden[section_id].transpose(1, 0, 2, 3)

        def one_expert(inputs):
            cot, hid, weight = inputs
            dh = jnp.einsum('dsk,hk->dsh', cot.astype(jnp.float32), weight.astype(jnp.float32)).astype(jnp.bfloat16)

            def add_group(total, pair):
                term = jnp.dot(pair[1].T, pair[0], preferred_element_type=jnp.float32).astype(jnp.bfloat16)
                term = lax.optimization_barrier(term)
                return total + term.astype(jnp.float32), None

            total, _ = lax.scan(add_group, jnp.zeros((H, D), jnp.float32), (cot, hid))
            return dh, total

        dh_all, dw_all = lax.map(one_expert, (scaled, saved, w_down[section_id]))
        hidden_grads.append(dh_all.transpose(1, 0, 2, 3))
        weight_grads.append(dw_all)
    return jnp.stack(hidden_grads), jnp.stack(weight_grads)
```

```python
import jax
import jax.numpy as jnp
from jax import lax
from jax.sharding import PartitionSpec as P


def shifted(value, axis, steps):
    count = lax.axis_size(axis)
    pairs = [(source, (source + steps) % count) for source in range(count)]
    return lax.ppermute(value, axis, pairs)


def dispatch_block(rows, ids, weights, count, width):
    flat_ids = ids.reshape(-1)
    onehot = (flat_ids[:, None] == jnp.arange(count, dtype=jnp.int32)[None, :]).astype(jnp.int32)
    position = jnp.sum((jnp.cumsum(onehot, axis=0) - 1) * onehot, axis=1)
    target = flat_ids * width + position
    scaled = (weights[:, :, None] * rows[:, None, :].astype(jnp.float32)).astype(jnp.bfloat16)
    scaled = scaled.reshape(-1, rows.shape[1])
    buffer = jnp.zeros((count * width, rows.shape[1]), jnp.bfloat16).at[target].set(scaled)
    return buffer.reshape(count, width, rows.shape[1])


def line_weight_grad(saved, scaled, chunks):
    d = lax.axis_index("dp")
    hid = saved.shape[1]
    blk = hid // 4
    width = scaled.shape[1] // chunks
    ends = [(0, 1), (3, 2)]
    hsend = lax.dynamic_slice_in_dim(saved, jnp.where(d == 0, blk, 0), hid - blk, axis=1)
    hrecv = lax.ppermute(hsend, "dp", ends)
    hfull = lax.dynamic_update_slice_in_dim(
        jnp.zeros_like(saved), hrecv, jnp.where(d == 1, blk, 0), axis=1
    )
    lhs = jnp.concatenate([saved, hfull], axis=0)
    row2 = jnp.where(d == 1, 2 * blk, 0)
    row3a = jnp.where(d == 1, 0, 3 * blk)
    row3b = jnp.where(d == 1, 0, blk)
    own = d * blk
    half = jnp.where(d == 1, blk, 0)
    edge = (d == 0) | (d == 3)
    pieces = []
    for c in range(chunks):
        sc = scaled[:, c * width:(c + 1) * width]
        srecv = lax.ppermute(sc, "dp", ends)
        rhs = jnp.concatenate([sc, srecv], axis=0)
        acc = lax.dot_general(
            lhs, rhs, (((0,), (0,)), ((), ())), preferred_element_type=jnp.float32
        )
        s2 = lax.dynamic_slice_in_dim(acc, row2, 2 * blk, axis=0).astype(jnp.bfloat16)
        r2 = lax.ppermute(s2, "dp", [(1, 2), (2, 1)])
        s3 = (
            lax.dynamic_slice_in_dim(acc, row3a, blk, axis=0)
            + lax.dynamic_slice_in_dim(r2, row3b, blk, axis=0).astype(jnp.float32)
        ).astype(jnp.bfloat16)
        r3 = lax.ppermute(s3, "dp", [(1, 0), (2, 3)])
        extra = jnp.where(edge, r3, lax.dynamic_slice_in_dim(r2, half, blk, axis=0))
        pieces.append(
            lax.dynamic_slice_in_dim(acc, own, blk, axis=0) + extra.astype(jnp.float32)
        )
    return jnp.concatenate(pieces, axis=1)


def shards(grad_out, routes, gates, hidden, w_down):
    incoming = shifted(grad_out, "section", -1)[0]
    groups = lax.axis_size("expert")
    saved = hidden[0, 0, 0]
    weight = w_down[0, 0]
    slot_count = saved.shape[0]
    width = slot_count // groups
    model_width = incoming.shape[1]
    outgoing = dispatch_block(incoming, routes[0], gates[0], groups, width)
    piece = lax.all_to_all(outgoing, "expert", split_axis=0, concat_axis=0, tiled=True)
    grad_rows_out = jnp.einsum(
        "skd,hd->skh", piece, weight, preferred_element_type=jnp.float32
    ).astype(jnp.bfloat16)
    scaled = piece.reshape(slot_count, model_width)
    if lax.axis_size("dp") == 4 and saved.shape[1] % 4 == 0:
        weight_grad = line_weight_grad(saved, scaled, 4)
    else:
        full = lax.dot_general(
            saved, scaled, (((0,), (0,)), ((), ())), preferred_element_type=jnp.float32
        )
        weight_grad = lax.psum_scatter(
            full.astype(jnp.bfloat16), "dp", scatter_dimension=0, tiled=True
        ).astype(jnp.float32)
    grad_hidden = grad_rows_out.reshape(1, 1, 1, slot_count, saved.shape[1])
    return (grad_hidden, weight_grad.reshape(1, 1, weight_grad.shape[0], model_width))


def solution(mesh):
    placed = (
        P("section", ("dp", "expert"), None),
        P("section", ("dp", "expert"), None),
        P("section", ("dp", "expert"), None),
        P("section", "dp", "expert", None, None),
        P("section", "expert", None, None),
    )
    return jax.shard_map(
        shards,
        mesh=mesh,
        in_specs=placed,
        out_specs=(P("section", "dp", "expert", None, None), P("section", "expert", "dp", None)),
        check_vma=False,
    )
```

```python
import jax
import jax.numpy as jnp
from jax import lax
from jax.sharding import PartitionSpec as P


def shifted(value, axis, steps):
    count = lax.axis_size(axis)
    pairs = [(source, (source + steps) % count) for source in range(count)]
    return lax.ppermute(value, axis, pairs)


def dispatch_targets(ids, count, width):
    flat_ids = ids.reshape(-1)
    onehot = (flat_ids[:, None] == jnp.arange(count, dtype=jnp.int32)[None, :]).astype(jnp.int32)
    position = jnp.sum((jnp.cumsum(onehot, axis=0) - 1) * onehot, axis=1)
    return flat_ids * width + position


def dispatch_rows(rows, weights, target, count, width):
    scaled = (weights[:, :, None] * rows[:, None, :].astype(jnp.float32)).astype(jnp.bfloat16)
    scaled = scaled.reshape(-1, rows.shape[1])
    buffer = jnp.zeros((count * width, rows.shape[1]), jnp.bfloat16).at[target].set(scaled)
    return buffer.reshape(count, width, rows.shape[1])


def line_weight_grad(saved, parts):
    d = lax.axis_index("dp")
    hid = saved.shape[1]
    blk = hid // 4
    ends = [(0, 1), (3, 2)]
    column_block = lax.broadcasted_iota(jnp.int32, saved.shape, 1) // blk
    hsend = jnp.where(column_block == d, jnp.zeros_like(saved), saved)
    hfull = lax.ppermute(hsend, "dp", ends)
    lhs = jnp.concatenate([saved, hfull], axis=0)
    row2 = jnp.where(d == 1, 2 * blk, 0)
    row3a = jnp.where(d == 1, 0, 3 * blk)
    row3b = jnp.where(d == 1, 0, blk)
    own = d * blk
    half = jnp.where(d == 1, blk, 0)
    edge = (d == 0) | (d == 3)
    pieces = []
    for sc in parts:
        srecv = lax.ppermute(sc, "dp", ends)
        rhs = jnp.concatenate([sc, srecv], axis=0)
        acc = lax.dot_general(
            lhs, rhs, (((0,), (0,)), ((), ())), preferred_element_type=jnp.float32
        )
        s2 = lax.dynamic_slice_in_dim(acc, row2, 2 * blk, axis=0).astype(jnp.bfloat16)
        r2 = lax.ppermute(s2, "dp", [(1, 2), (2, 1)])
        s3 = (
            lax.dynamic_slice_in_dim(acc, row3a, blk, axis=0)
            + lax.dynamic_slice_in_dim(r2, row3b, blk, axis=0).astype(jnp.float32)
        ).astype(jnp.bfloat16)
        r3 = lax.ppermute(s3, "dp", [(1, 0), (2, 3)])
        extra = jnp.where(edge, r3, lax.dynamic_slice_in_dim(r2, half, blk, axis=0))
        pieces.append(
            lax.dynamic_slice_in_dim(acc, own, blk, axis=0) + extra.astype(jnp.float32)
        )
    return jnp.concatenate(pieces, axis=1)


def shards(grad_out, routes, gates, hidden, w_down):
    groups = lax.axis_size("expert")
    saved = hidden[0, 0, 0]
    weight = w_down[0, 0]
    slot_count = saved.shape[0]
    width = slot_count // groups
    model_width = grad_out.shape[2]
    chunks = 4 if model_width % 512 == 0 else 1
    step = model_width // chunks
    target = dispatch_targets(routes[0], groups, width)
    parts = []
    for c in range(chunks):
        rows = shifted(grad_out[0, :, c * step:(c + 1) * step], "section", -1)
        outgoing = dispatch_rows(rows, gates[0], target, groups, width)
        piece = lax.all_to_all(outgoing, "expert", split_axis=0, concat_axis=0, tiled=True)
        parts.append(piece.reshape(slot_count, step))
    scaled = jnp.concatenate(parts, axis=1)
    grad_rows_out = jnp.einsum(
        "sd,hd->sh", scaled, weight, preferred_element_type=jnp.float32
    ).astype(jnp.bfloat16)
    if lax.axis_size("dp") == 4 and saved.shape[1] % 4 == 0:
        weight_grad = line_weight_grad(saved, parts)
    else:
        full = lax.dot_general(
            saved, scaled, (((0,), (0,)), ((), ())), preferred_element_type=jnp.float32
        )
        weight_grad = lax.psum_scatter(
            full.astype(jnp.bfloat16), "dp", scatter_dimension=0, tiled=True
        ).astype(jnp.float32)
    grad_hidden = grad_rows_out.reshape(1, 1, 1, slot_count, saved.shape[1])
    return (grad_hidden, weight_grad.reshape(1, 1, weight_grad.shape[0], model_width))


def solution(mesh):
    placed = (
        P("section", ("dp", "expert"), None),
        P("section", ("dp", "expert"), None),
        P("section", ("dp", "expert"), None),
        P("section", "dp", "expert", None, None),
        P("section", "expert", None, None),
    )
    return jax.shard_map(
        shards,
        mesh=mesh,
        in_specs=placed,
        out_specs=(P("section", "dp", "expert", None, None), P("section", "expert", "dp", None)),
        check_vma=False,
    )
```

```python
import jax
import jax.numpy as jnp
from jax import lax
from jax.sharding import PartitionSpec as P


def shifted(value, axis, steps):
    count = lax.axis_size(axis)
    pairs = [(source, (source + steps) % count) for source in range(count)]
    return lax.ppermute(value, axis, pairs)


def dispatch_targets(ids, count, width):
    flat_ids = ids.reshape(-1)
    onehot = (flat_ids[:, None] == jnp.arange(count, dtype=jnp.int32)[None, :]).astype(jnp.int32)
    position = jnp.sum((jnp.cumsum(onehot, axis=0) - 1) * onehot, axis=1)
    return flat_ids * width + position


def dispatch_rows(rows, weights, target, count, width):
    scaled = (weights[:, :, None] * rows[:, None, :].astype(jnp.float32)).astype(jnp.bfloat16)
    scaled = scaled.reshape(-1, rows.shape[1])
    buffer = jnp.zeros((count * width, rows.shape[1]), jnp.bfloat16).at[target].set(scaled)
    return buffer.reshape(count, width, rows.shape[1])


def line_weight_grad(saved, parts):
    d = lax.axis_index("dp")
    hid = saved.shape[1]
    blk = hid // 4
    ends = [(0, 1), (3, 2)]
    column_block = lax.broadcasted_iota(jnp.int32, saved.shape, 1) // blk
    hsend = jnp.where(column_block == d, jnp.zeros_like(saved), saved)
    hfull = lax.ppermute(hsend, "dp", ends)
    lhs = jnp.concatenate([saved, hfull], axis=0)
    row2 = jnp.where(d == 1, 2 * blk, 0)
    row3a = jnp.where(d == 1, 0, 3 * blk)
    row3b = jnp.where(d == 1, 0, blk)
    own = d * blk
    half = jnp.where(d == 1, blk, 0)
    edge = (d == 0) | (d == 3)
    pieces = []
    for sc in parts:
        srecv = lax.ppermute(sc, "dp", ends)
        rhs = jnp.concatenate([sc, srecv], axis=0)
        acc = lax.dot_general(
            lhs, rhs, (((0,), (0,)), ((), ())), preferred_element_type=jnp.float32
        )
        s2 = lax.dynamic_slice_in_dim(acc, row2, 2 * blk, axis=0).astype(jnp.bfloat16)
        r2 = lax.ppermute(s2, "dp", [(1, 2), (2, 1)])
        s3 = (
            lax.dynamic_slice_in_dim(acc, row3a, blk, axis=0)
            + lax.dynamic_slice_in_dim(r2, row3b, blk, axis=0).astype(jnp.float32)
        ).astype(jnp.bfloat16)
        r3 = lax.ppermute(s3, "dp", [(1, 0), (2, 3)])
        extra = jnp.where(edge, r3, lax.dynamic_slice_in_dim(r2, half, blk, axis=0))
        pieces.append(
            lax.dynamic_slice_in_dim(acc, own, blk, axis=0) + extra.astype(jnp.float32)
        )
    return jnp.concatenate(pieces, axis=1)


def shards(grad_out, routes, gates, hidden, w_down):
    groups = lax.axis_size("expert")
    saved = hidden[0, 0, 0]
    weight = w_down[0, 0]
    slot_count = saved.shape[0]
    width = slot_count // groups
    model_width = grad_out.shape[2]
    target = dispatch_targets(routes[0], groups, width)
    incoming = shifted(grad_out, "section", -1)[0]
    outgoing = dispatch_rows(incoming, gates[0], target, groups, width)
    piece = lax.all_to_all(outgoing, "expert", split_axis=0, concat_axis=0, tiled=True)
    scaled = piece.reshape(slot_count, model_width)
    chunks = 8 if model_width % 2048 == 0 else 1
    step = model_width // chunks
    parts = [scaled[:, c * step:(c + 1) * step] for c in range(chunks)]
    grad_rows_out = jnp.einsum(
        "sd,hd->sh", scaled, weight, preferred_element_type=jnp.float32
    ).astype(jnp.bfloat16)
    if lax.axis_size("dp") == 4 and saved.shape[1] % 4 == 0:
        weight_grad = line_weight_grad(saved, parts)
    else:
        full = lax.dot_general(
            saved, scaled, (((0,), (0,)), ((), ())), preferred_element_type=jnp.float32
        )
        weight_grad = lax.psum_scatter(
            full.astype(jnp.bfloat16), "dp", scatter_dimension=0, tiled=True
        ).astype(jnp.float32)
    grad_hidden = grad_rows_out.reshape(1, 1, 1, slot_count, saved.shape[1])
    return (grad_hidden, weight_grad.reshape(1, 1, weight_grad.shape[0], model_width))


def solution(mesh):
    placed = (
        P("section", ("dp", "expert"), None),
        P("section", ("dp", "expert"), None),
        P("section", ("dp", "expert"), None),
        P("section", "dp", "expert", None, None),
        P("section", "expert", None, None),
    )
    return jax.shard_map(
        shards,
        mesh=mesh,
        in_specs=placed,
        out_specs=(P("section", "dp", "expert", None, None), P("section", "expert", "dp", None)),
        check_vma=False,
    )
```

```python
import jax
import jax.numpy as jnp
from jax import lax
from jax.sharding import PartitionSpec as P


def shifted(value, axis, steps):
    count = lax.axis_size(axis)
    pairs = [(source, (source + steps) % count) for source in range(count)]
    return lax.ppermute(value, axis, pairs)


def dispatch_targets(ids, count, width):
    flat_ids = ids.reshape(-1)
    onehot = (flat_ids[:, None] == jnp.arange(count, dtype=jnp.int32)[None, :]).astype(jnp.int32)
    position = jnp.sum((jnp.cumsum(onehot, axis=0) - 1) * onehot, axis=1)
    return (flat_ids * width + position).reshape(ids.shape)


def dispatch_rows(rows, weights, target, count, width):
    slots = count * width
    total = None
    for k in range(target.shape[1]):
        scaled = (weights[:, k:k + 1] * rows.astype(jnp.float32)).astype(jnp.bfloat16)
        onehot = lax.broadcasted_iota(jnp.int32, (slots, rows.shape[0]), 0) == target[None, :, k]
        term = jnp.dot(onehot.astype(jnp.bfloat16), scaled, preferred_element_type=jnp.float32)
        total = term if total is None else total + term
    return total.astype(jnp.bfloat16).reshape(count, width, rows.shape[1])


def send_hidden(saved):
    d = lax.axis_index("dp")
    blk = saved.shape[1] // 4
    column_block = lax.broadcasted_iota(jnp.int32, saved.shape, 1) // blk
    hsend = jnp.where(column_block == d, jnp.zeros_like(saved), saved)
    return lax.ppermute(hsend, "dp", [(0, 1), (3, 2)])


def line_weight_grad(saved, hfull, scaled, chunks):
    d = lax.axis_index("dp")
    hid = saved.shape[1]
    blk = hid // 4
    width = scaled.shape[1] // chunks
    ends = [(0, 1), (3, 2)]
    lhs = jnp.concatenate([saved, hfull], axis=0)
    row2 = jnp.where(d == 1, 2 * blk, 0)
    row3a = jnp.where(d == 1, 0, 3 * blk)
    row3b = jnp.where(d == 1, 0, blk)
    own = d * blk
    half = jnp.where(d == 1, blk, 0)
    edge = (d == 0) | (d == 3)
    pieces = []
    for c in range(chunks):
        sc = scaled[:, c * width:(c + 1) * width]
        srecv = lax.ppermute(sc, "dp", ends)
        rhs = jnp.concatenate([sc, srecv], axis=0)
        acc = lax.dot_general(
            lhs, rhs, (((0,), (0,)), ((), ())), preferred_element_type=jnp.float32
        )
        s2 = lax.dynamic_slice_in_dim(acc, row2, 2 * blk, axis=0).astype(jnp.bfloat16)
        r2 = lax.ppermute(s2, "dp", [(1, 2), (2, 1)])
        s3 = (
            lax.dynamic_slice_in_dim(acc, row3a, blk, axis=0)
            + lax.dynamic_slice_in_dim(r2, row3b, blk, axis=0).astype(jnp.float32)
        ).astype(jnp.bfloat16)
        r3 = lax.ppermute(s3, "dp", [(1, 0), (2, 3)])
        extra = jnp.where(edge, r3, lax.dynamic_slice_in_dim(r2, half, blk, axis=0))
        pieces.append(
            lax.dynamic_slice_in_dim(acc, own, blk, axis=0) + extra.astype(jnp.float32)
        )
    return jnp.concatenate(pieces, axis=1), s2


def shards(grad_out, routes, gates, hidden, w_down):
    incoming = shifted(grad_out, "section", -1)[0]
    groups = lax.axis_size("expert")
    saved = hidden[0, 0, 0]
    weight = w_down[0, 0]
    slot_count = saved.shape[0]
    width = slot_count // groups
    model_width = incoming.shape[1]
    target = dispatch_targets(routes[0], groups, width)
    outgoing = dispatch_rows(incoming, gates[0], target, groups, width)
    line = lax.axis_size("dp") == 4 and saved.shape[1] % 4 == 0
    if line:
        hfull = send_hidden(saved)
        outgoing, hfull = lax.optimization_barrier((outgoing, hfull))
    piece = lax.all_to_all(outgoing, "expert", split_axis=0, concat_axis=0, tiled=True)
    scaled = piece.reshape(slot_count, model_width)
    if line:
        weight_grad, anchor = line_weight_grad(saved, hfull, scaled, 4)
        late, _ = lax.optimization_barrier((scaled, anchor))
    else:
        full = lax.dot_general(
            saved, scaled, (((0,), (0,)), ((), ())), preferred_element_type=jnp.float32
        )
        weight_grad = lax.psum_scatter(
            full.astype(jnp.bfloat16), "dp", scatter_dimension=0, tiled=True
        ).astype(jnp.float32)
        late = scaled
    grad_rows_out = jnp.einsum(
        "sd,hd->sh", late, weight, preferred_element_type=jnp.float32
    ).astype(jnp.bfloat16)
    grad_hidden = grad_rows_out.reshape(1, 1, 1, slot_count, saved.shape[1])
    return (grad_hidden, weight_grad.reshape(1, 1, weight_grad.shape[0], model_width))


def solution(mesh):
    placed = (
        P("section", ("dp", "expert"), None),
        P("section", ("dp", "expert"), None),
        P("section", ("dp", "expert"), None),
        P("section", "dp", "expert", None, None),
        P("section", "expert", None, None),
    )
    return jax.shard_map(
        shards,
        mesh=mesh,
        in_specs=placed,
        out_specs=(P("section", "dp", "expert", None, None), P("section", "expert", "dp", None)),
        check_vma=False,
    )
```

```python
import jax
import jax.numpy as jnp
from jax import lax
from jax.sharding import PartitionSpec as P


def shifted(value, axis, steps):
    count = lax.axis_size(axis)
    pairs = [(source, (source + steps) % count) for source in range(count)]
    return lax.ppermute(value, axis, pairs)


def dispatch_targets(ids, count, width):
    flat_ids = ids.reshape(-1)
    onehot = (flat_ids[:, None] == jnp.arange(count, dtype=jnp.int32)[None, :]).astype(jnp.int32)
    position = jnp.sum((jnp.cumsum(onehot, axis=0) - 1) * onehot, axis=1)
    return (flat_ids * width + position).reshape(ids.shape)


def dispatch_rows(rows, weights, target, count, width):
    slots = count * width
    total = None
    for k in range(target.shape[1]):
        scaled = (weights[:, k:k + 1] * rows.astype(jnp.float32)).astype(jnp.bfloat16)
        onehot = lax.broadcasted_iota(jnp.int32, (slots, rows.shape[0]), 0) == target[None, :, k]
        term = jnp.dot(onehot.astype(jnp.bfloat16), scaled, preferred_element_type=jnp.float32)
        total = term if total is None else total + term
    return total.astype(jnp.bfloat16).reshape(count, width, rows.shape[1])


def send_hidden(saved):
    d = lax.axis_index("dp")
    blk = saved.shape[1] // 4
    column_block = lax.broadcasted_iota(jnp.int32, saved.shape, 1) // blk
    hsend = jnp.where(column_block == d, jnp.zeros_like(saved), saved)
    return lax.ppermute(hsend, "dp", [(0, 1), (3, 2)])


def line_weight_grad(saved, hfull, scaled):
    d = lax.axis_index("dp")
    hid = saved.shape[1]
    blk = hid // 4
    model_width = scaled.shape[1]
    if model_width % 2048 == 0:
        unit = model_width // 8
        widths = [unit, 3 * unit, 3 * unit, unit]
    else:
        widths = [model_width]
    ends = [(0, 1), (3, 2)]
    lhs = jnp.concatenate([saved, hfull], axis=0)
    row2 = jnp.where(d == 1, 2 * blk, 0)
    row3a = jnp.where(d == 1, 0, 3 * blk)
    row3b = jnp.where(d == 1, 0, blk)
    own = d * blk
    half = jnp.where(d == 1, blk, 0)
    edge = (d == 0) | (d == 3)
    pieces = []
    srecv = None
    landed = []
    begin = 0
    for width in widths:
        sc = scaled[:, begin:begin + width]
        begin += width
        sent = sc
        if srecv is not None:
            sent, _ = lax.optimization_barrier((sc, srecv))
        srecv = lax.ppermute(sent, "dp", ends)
        rhs = jnp.concatenate([sc, srecv], axis=0)
        acc = lax.dot_general(
            lhs, rhs, (((0,), (0,)), ((), ())), preferred_element_type=jnp.float32
        )
        s2 = lax.dynamic_slice_in_dim(acc, row2, 2 * blk, axis=0).astype(jnp.bfloat16)
        if len(landed) >= 2:
            s2, _ = lax.optimization_barrier((s2, landed[-2]))
        r2 = lax.ppermute(s2, "dp", [(1, 2), (2, 1)])
        landed.append(r2)
        s3 = (
            lax.dynamic_slice_in_dim(acc, row3a, blk, axis=0)
            + lax.dynamic_slice_in_dim(r2, row3b, blk, axis=0).astype(jnp.float32)
        ).astype(jnp.bfloat16)
        r3 = lax.ppermute(s3, "dp", [(1, 0), (2, 3)])
        extra = jnp.where(edge, r3, lax.dynamic_slice_in_dim(r2, half, blk, axis=0))
        pieces.append(
            lax.dynamic_slice_in_dim(acc, own, blk, axis=0) + extra.astype(jnp.float32)
        )
    return jnp.concatenate(pieces, axis=1), s2


def shards(grad_out, routes, gates, hidden, w_down):
    incoming = shifted(grad_out, "section", -1)[0]
    groups = lax.axis_size("expert")
    saved = hidden[0, 0, 0]
    weight = w_down[0, 0]
    slot_count = saved.shape[0]
    width = slot_count // groups
    model_width = incoming.shape[1]
    target = dispatch_targets(routes[0], groups, width)
    outgoing = dispatch_rows(incoming, gates[0], target, groups, width)
    line = lax.axis_size("dp") == 4 and saved.shape[1] % 4 == 0
    if line:
        hfull = send_hidden(saved)
    piece = lax.all_to_all(outgoing, "expert", split_axis=0, concat_axis=0, tiled=True)
    scaled = piece.reshape(slot_count, model_width)
    if line:
        scaled, hfull = lax.optimization_barrier((scaled, hfull))
    if line:
        weight_grad, anchor = line_weight_grad(saved, hfull, scaled)
        late, _ = lax.optimization_barrier((scaled, anchor))
    else:
        full = lax.dot_general(
            saved, scaled, (((0,), (0,)), ((), ())), preferred_element_type=jnp.float32
        )
        weight_grad = lax.psum_scatter(
            full.astype(jnp.bfloat16), "dp", scatter_dimension=0, tiled=True
        ).astype(jnp.float32)
        late = scaled
    grad_rows_out = jnp.einsum(
        "sd,hd->sh", late, weight, preferred_element_type=jnp.float32
    ).astype(jnp.bfloat16)
    grad_hidden = grad_rows_out.reshape(1, 1, 1, slot_count, saved.shape[1])
    return (grad_hidden, weight_grad.reshape(1, 1, weight_grad.shape[0], model_width))


def solution(mesh):
    placed = (
        P("section", ("dp", "expert"), None),
        P("section", ("dp", "expert"), None),
        P("section", ("dp", "expert"), None),
        P("section", "dp", "expert", None, None),
        P("section", "expert", None, None),
    )
    return jax.shard_map(
        shards,
        mesh=mesh,
        in_specs=placed,
        out_specs=(P("section", "dp", "expert", None, None), P("section", "expert", "dp", None)),
        check_vma=False,
    )
```

```python
import jax
import jax.numpy as jnp
from jax import lax
from jax.sharding import PartitionSpec as P


def shifted(value, axis, steps):
    count = lax.axis_size(axis)
    pairs = [(source, (source + steps) % count) for source in range(count)]
    return lax.ppermute(value, axis, pairs)


def dispatch_targets(ids, count, width):
    flat_ids = ids.reshape(-1)
    onehot = (flat_ids[:, None] == jnp.arange(count, dtype=jnp.int32)[None, :]).astype(jnp.int32)
    position = jnp.sum((jnp.cumsum(onehot, axis=0) - 1) * onehot, axis=1)
    return (flat_ids * width + position).reshape(ids.shape)


def dispatch_rows(rows, weights, target, count, width):
    slots = count * width
    total = None
    for k in range(target.shape[1]):
        scaled = (weights[:, k:k + 1] * rows.astype(jnp.float32)).astype(jnp.bfloat16)
        onehot = lax.broadcasted_iota(jnp.int32, (slots, rows.shape[0]), 0) == target[None, :, k]
        term = jnp.dot(onehot.astype(jnp.bfloat16), scaled, preferred_element_type=jnp.float32)
        total = term if total is None else total + term
    return total.astype(jnp.bfloat16).reshape(count, width, rows.shape[1])


def send_hidden(saved):
    d = lax.axis_index("dp")
    blk = saved.shape[1] // 4
    column_block = lax.broadcasted_iota(jnp.int32, saved.shape, 1) // blk
    hsend = jnp.where(column_block == d, jnp.zeros_like(saved), saved)
    return lax.ppermute(hsend, "dp", [(0, 1), (3, 2)])


def line_weight_grad(saved, hfull, scaled, chunks):
    d = lax.axis_index("dp")
    hid = saved.shape[1]
    blk = hid // 4
    width = scaled.shape[1] // chunks
    ends = [(0, 1), (3, 2)]
    lhs = jnp.concatenate([saved, hfull], axis=0)
    row2 = jnp.where(d == 1, 2 * blk, 0)
    row3a = jnp.where(d == 1, 0, 3 * blk)
    row3b = jnp.where(d == 1, 0, blk)
    own = d * blk
    half = jnp.where(d == 1, blk, 0)
    edge = (d == 0) | (d == 3)
    pieces = []
    for c in range(chunks):
        sc = scaled[:, c * width:(c + 1) * width]
        srecv = lax.ppermute(sc, "dp", ends)
        rhs = jnp.concatenate([sc, srecv], axis=0)
        acc = lax.dot_general(
            lhs, rhs, (((0,), (0,)), ((), ())), preferred_element_type=jnp.float32
        )
        s2 = lax.dynamic_slice_in_dim(acc, row2, 2 * blk, axis=0).astype(jnp.bfloat16)
        r2 = lax.ppermute(s2, "dp", [(1, 2), (2, 1)])
        s3 = (
            lax.dynamic_slice_in_dim(acc, row3a, blk, axis=0)
            + lax.dynamic_slice_in_dim(r2, row3b, blk, axis=0).astype(jnp.float32)
        ).astype(jnp.bfloat16)
        r3 = lax.ppermute(s3, "dp", [(1, 0), (2, 3)])
        extra = jnp.where(edge, r3, lax.dynamic_slice_in_dim(r2, half, blk, axis=0))
        pieces.append(
            lax.dynamic_slice_in_dim(acc, own, blk, axis=0) + extra.astype(jnp.float32)
        )
    return jnp.concatenate(pieces, axis=1), s2


def shards(grad_out, routes, gates, hidden, w_down):
    incoming = shifted(grad_out, "section", -1)[0]
    groups = lax.axis_size("expert")
    saved = hidden[0, 0, 0]
    weight = w_down[0, 0]
    slot_count = saved.shape[0]
    width = slot_count // groups
    model_width = incoming.shape[1]
    target = dispatch_targets(routes[0], groups, width)
    outgoing = dispatch_rows(incoming, gates[0], target, groups, width)
    line = lax.axis_size("dp") == 4 and saved.shape[1] % 4 == 0
    if line:
        hfull = send_hidden(saved)
    piece = lax.all_to_all(outgoing, "expert", split_axis=0, concat_axis=0, tiled=True)
    scaled = piece.reshape(slot_count, model_width)
    if line:
        weight_grad, anchor = line_weight_grad(saved, hfull, scaled, 4)
        late, _ = lax.optimization_barrier((scaled, anchor))
    else:
        full = lax.dot_general(
            saved, scaled, (((0,), (0,)), ((), ())), preferred_element_type=jnp.float32
        )
        weight_grad = lax.psum_scatter(
            full.astype(jnp.bfloat16), "dp", scatter_dimension=0, tiled=True
        ).astype(jnp.float32)
        late = scaled
    grad_rows_out = jnp.einsum(
        "sd,hd->sh", late, weight, preferred_element_type=jnp.float32
    ).astype(jnp.bfloat16)
    grad_hidden = grad_rows_out.reshape(1, 1, 1, slot_count, saved.shape[1])
    return (grad_hidden, weight_grad.reshape(1, 1, weight_grad.shape[0], model_width))


def solution(mesh):
    placed = (
        P("section", ("dp", "expert"), None),
        P("section", ("dp", "expert"), None),
        P("section", ("dp", "expert"), None),
        P("section", "dp", "expert", None, None),
        P("section", "expert", None, None),
    )
    return jax.shard_map(
        shards,
        mesh=mesh,
        in_specs=placed,
        out_specs=(P("section", "dp", "expert", None, None), P("section", "expert", "dp", None)),
        check_vma=False,
    )
```

```python
import jax
import jax.numpy as jnp
from jax import lax
from jax.sharding import PartitionSpec as P


def shifted(value, axis, steps):
    count = lax.axis_size(axis)
    pairs = [(source, (source + steps) % count) for source in range(count)]
    return lax.ppermute(value, axis, pairs)


def dispatch_targets(ids, count, width):
    flat_ids = ids.reshape(-1)
    onehot = (flat_ids[:, None] == jnp.arange(count, dtype=jnp.int32)[None, :]).astype(jnp.int32)
    position = jnp.sum((jnp.cumsum(onehot, axis=0) - 1) * onehot, axis=1)
    return (flat_ids * width + position).reshape(ids.shape)


def dispatch_rows(rows, weights, target, count, width):
    slots = count * width
    total = None
    for k in range(target.shape[1]):
        scaled = (weights[:, k:k + 1] * rows.astype(jnp.float32)).astype(jnp.bfloat16)
        onehot = lax.broadcasted_iota(jnp.int32, (slots, rows.shape[0]), 0) == target[None, :, k]
        term = jnp.dot(onehot.astype(jnp.bfloat16), scaled, preferred_element_type=jnp.float32)
        total = term if total is None else total + term
    return total.astype(jnp.bfloat16).reshape(count, width, rows.shape[1])


def send_hidden(saved):
    d = lax.axis_index("dp")
    blk = saved.shape[1] // 4
    column_block = lax.broadcasted_iota(jnp.int32, saved.shape, 1) // blk
    hsend = jnp.where(column_block == d, jnp.zeros_like(saved), saved)
    return lax.ppermute(hsend, "dp", [(0, 1), (3, 2)])


def line_weight_grad(saved, hfull, scaled, chunks):
    d = lax.axis_index("dp")
    hid = saved.shape[1]
    blk = hid // 4
    width = scaled.shape[1] // chunks
    ends = [(0, 1), (3, 2)]
    lhs = jnp.concatenate([saved, hfull], axis=0)
    row2 = jnp.where(d == 1, 2 * blk, 0)
    row3a = jnp.where(d == 1, 0, 3 * blk)
    row3b = jnp.where(d == 1, 0, blk)
    own = d * blk
    half = jnp.where(d == 1, blk, 0)
    edge = (d == 0) | (d == 3)

    def finish(acc, r2, after):
        part = (
            lax.dynamic_slice_in_dim(acc, row3a, blk, axis=0)
            + lax.dynamic_slice_in_dim(r2, row3b, blk, axis=0).astype(jnp.float32)
        )
        if after is not None:
            part, _ = lax.optimization_barrier((part, after))
        r3 = lax.ppermute(part.astype(jnp.bfloat16), "dp", [(1, 0), (2, 3)])
        extra = jnp.where(edge, r3, lax.dynamic_slice_in_dim(r2, half, blk, axis=0))
        return lax.dynamic_slice_in_dim(acc, own, blk, axis=0) + extra.astype(jnp.float32)

    first = lax.ppermute(scaled[:, :width], "dp", ends)
    second, _ = lax.optimization_barrier((scaled[:, width:2 * width], first))
    second = lax.ppermute(second, "dp", ends)
    rest, _ = lax.optimization_barrier((scaled[:, 2 * width:], second))
    rest = lax.ppermute(rest, "dp", ends)
    received = [first, second] + [rest[:, c * width:(c + 1) * width] for c in range(chunks - 2)]
    pieces = []
    held = None
    for c in range(chunks):
        sc = scaled[:, c * width:(c + 1) * width]
        rhs = jnp.concatenate([sc, received[c]], axis=0)
        acc = lax.dot_general(
            lhs, rhs, (((0,), (0,)), ((), ())), preferred_element_type=jnp.float32
        )
        s2 = lax.dynamic_slice_in_dim(acc, row2, 2 * blk, axis=0).astype(jnp.bfloat16)
        r2 = lax.ppermute(s2, "dp", [(1, 2), (2, 1)])
        if held is not None:
            pieces.append(finish(*held, s2))
        held = (acc, r2)
    pieces.append(finish(*held, None))
    return jnp.concatenate(pieces, axis=1), s2


def shards(grad_out, routes, gates, hidden, w_down):
    incoming = shifted(grad_out, "section", -1)[0]
    groups = lax.axis_size("expert")
    saved = hidden[0, 0, 0]
    weight = w_down[0, 0]
    slot_count = saved.shape[0]
    width = slot_count // groups
    model_width = incoming.shape[1]
    target = dispatch_targets(routes[0], groups, width)
    outgoing = dispatch_rows(incoming, gates[0], target, groups, width)
    line = lax.axis_size("dp") == 4 and saved.shape[1] % 4 == 0
    if line:
        hfull = send_hidden(saved)
    piece = lax.all_to_all(outgoing, "expert", split_axis=0, concat_axis=0, tiled=True)
    scaled = piece.reshape(slot_count, model_width)
    if line:
        weight_grad, anchor = line_weight_grad(saved, hfull, scaled, 4)
        late, _ = lax.optimization_barrier((scaled, anchor))
    else:
        full = lax.dot_general(
            saved, scaled, (((0,), (0,)), ((), ())), preferred_element_type=jnp.float32
        )
        weight_grad = lax.psum_scatter(
            full.astype(jnp.bfloat16), "dp", scatter_dimension=0, tiled=True
        ).astype(jnp.float32)
        late = scaled
    grad_rows_out = jnp.einsum(
        "sd,hd->sh", late, weight, preferred_element_type=jnp.float32
    ).astype(jnp.bfloat16)
    grad_hidden = grad_rows_out.reshape(1, 1, 1, slot_count, saved.shape[1])
    return (grad_hidden, weight_grad.reshape(1, 1, weight_grad.shape[0], model_width))


def solution(mesh):
    placed = (
        P("section", ("dp", "expert"), None),
        P("section", ("dp", "expert"), None),
        P("section", ("dp", "expert"), None),
        P("section", "dp", "expert", None, None),
        P("section", "expert", None, None),
    )
    return jax.shard_map(
        shards,
        mesh=mesh,
        in_specs=placed,
        out_specs=(P("section", "dp", "expert", None, None), P("section", "expert", "dp", None)),
        check_vma=False,
    )
```

```python
import jax
import jax.numpy as jnp
from jax import lax
from jax.sharding import PartitionSpec as P


def shifted(value, axis, steps):
    count = lax.axis_size(axis)
    pairs = [(source, (source + steps) % count) for source in range(count)]
    return lax.ppermute(value, axis, pairs)


def dispatch_targets(ids, count, width):
    flat_ids = ids.reshape(-1)
    onehot = (flat_ids[:, None] == jnp.arange(count, dtype=jnp.int32)[None, :]).astype(jnp.int32)
    position = jnp.sum((jnp.cumsum(onehot, axis=0) - 1) * onehot, axis=1)
    return (flat_ids * width + position).reshape(ids.shape)


def dispatch_rows(rows, weights, target, count, width):
    slots = count * width
    total = None
    for k in range(target.shape[1]):
        scaled = (weights[:, k:k + 1] * rows.astype(jnp.float32)).astype(jnp.bfloat16)
        onehot = lax.broadcasted_iota(jnp.int32, (slots, rows.shape[0]), 0) == target[None, :, k]
        term = jnp.dot(onehot.astype(jnp.bfloat16), scaled, preferred_element_type=jnp.float32)
        total = term if total is None else total + term
    return total.astype(jnp.bfloat16).reshape(count, width, rows.shape[1])


def cols(array, start, size):
    return lax.dynamic_slice_in_dim(array, start, size, axis=1)


def line_weight_grad(saved, scaled, chunks):
    d = lax.axis_index("dp")
    blk = saved.shape[1] // 4
    inner = [(0, 1), (3, 2)]
    across = [(1, 2), (2, 1)]
    far = [(0, 2), (3, 1)]
    back = [(1, 0), (2, 3)]
    h_near = lax.ppermute(cols(saved, jnp.where(d == 0, blk, 2 * blk), blk), "dp", inner)
    h_far = lax.ppermute(cols(saved, jnp.where(d == 0, 2 * blk, 0), 2 * blk), "dp", far)
    h_mid = lax.ppermute(cols(saved, jnp.where(d == 1, 2 * blk, 0), 2 * blk), "dp", across)
    own_at = jnp.where(d == 1, blk, 0)
    end_at = jnp.where(d == 1, 0, blk)
    own_block = jnp.concatenate(
        [cols(saved, d * blk, blk), h_near, cols(h_mid, own_at, blk), cols(h_far, own_at, blk)], axis=0
    )
    end_block = jnp.concatenate(
        [cols(saved, jnp.where(d == 1, 0, 3 * blk), blk), jnp.zeros_like(h_near),
         cols(h_mid, end_at, blk), cols(h_far, end_at, blk)], axis=0
    )
    lhs = jnp.concatenate([own_block, end_block], axis=1)
    edge = (d == 0) | (d == 3)
    width = scaled.shape[1] // chunks
    pieces = []
    for c in range(chunks):
        sc = scaled[:, c * width:(c + 1) * width]
        rhs = jnp.concatenate(
            [sc, lax.ppermute(sc, "dp", inner), lax.ppermute(sc, "dp", across),
             lax.ppermute(sc, "dp", far)], axis=0
        )
        acc = lax.dot_general(
            lhs, rhs, (((0,), (0,)), ((), ())), preferred_element_type=jnp.float32
        )
        tail = lax.ppermute(acc[blk:].astype(jnp.bfloat16), "dp", back)
        pieces.append(acc[:blk] + jnp.where(edge, tail.astype(jnp.float32), 0.0))
    return jnp.concatenate(pieces, axis=1), tail


def shards(grad_out, routes, gates, hidden, w_down):
    incoming = shifted(grad_out, "section", -1)[0]
    groups = lax.axis_size("expert")
    saved = hidden[0, 0, 0]
    weight = w_down[0, 0]
    slot_count = saved.shape[0]
    width = slot_count // groups
    model_width = incoming.shape[1]
    target = dispatch_targets(routes[0], groups, width)
    outgoing = dispatch_rows(incoming, gates[0], target, groups, width)
    line = lax.axis_size("dp") == 4 and saved.shape[1] % 4 == 0
    piece = lax.all_to_all(outgoing, "expert", split_axis=0, concat_axis=0, tiled=True)
    scaled = piece.reshape(slot_count, model_width)
    if line:
        weight_grad, anchor = line_weight_grad(saved, scaled, 4)
        late, _ = lax.optimization_barrier((scaled, anchor))
    else:
        full = lax.dot_general(
            saved, scaled, (((0,), (0,)), ((), ())), preferred_element_type=jnp.float32
        )
        weight_grad = lax.psum_scatter(
            full.astype(jnp.bfloat16), "dp", scatter_dimension=0, tiled=True
        ).astype(jnp.float32)
        late = scaled
    grad_rows_out = jnp.einsum(
        "sd,hd->sh", late, weight, preferred_element_type=jnp.float32
    ).astype(jnp.bfloat16)
    grad_hidden = grad_rows_out.reshape(1, 1, 1, slot_count, saved.shape[1])
    return (grad_hidden, weight_grad.reshape(1, 1, weight_grad.shape[0], model_width))


def solution(mesh):
    placed = (
        P("section", ("dp", "expert"), None),
        P("section", ("dp", "expert"), None),
        P("section", ("dp", "expert"), None),
        P("section", "dp", "expert", None, None),
        P("section", "expert", None, None),
    )
    return jax.shard_map(
        shards,
        mesh=mesh,
        in_specs=placed,
        out_specs=(P("section", "dp", "expert", None, None), P("section", "expert", "dp", None)),
        check_vma=False,
    )
```

```python
import jax
import jax.numpy as jnp
from jax import lax
from jax.sharding import PartitionSpec as P


def shifted(value, axis, steps):
    count = lax.axis_size(axis)
    pairs = [(source, (source + steps) % count) for source in range(count)]
    return lax.ppermute(value, axis, pairs)


def dispatch_targets(ids, count, width):
    flat_ids = ids.reshape(-1)
    onehot = (flat_ids[:, None] == jnp.arange(count, dtype=jnp.int32)[None, :]).astype(jnp.int32)
    position = jnp.sum((jnp.cumsum(onehot, axis=0) - 1) * onehot, axis=1)
    return (flat_ids * width + position).reshape(ids.shape)


def dispatch_rows(rows, weights, target, count, width):
    slots = count * width
    total = None
    for k in range(target.shape[1]):
        scaled = (weights[:, k:k + 1] * rows.astype(jnp.float32)).astype(jnp.bfloat16)
        onehot = lax.broadcasted_iota(jnp.int32, (slots, rows.shape[0]), 0) == target[None, :, k]
        term = jnp.dot(onehot.astype(jnp.bfloat16), scaled, preferred_element_type=jnp.float32)
        total = term if total is None else total + term
    return total.astype(jnp.bfloat16).reshape(count, width, rows.shape[1])


def rows(array, start, size):
    return lax.dynamic_slice_in_dim(array, start, size, axis=0)


def hidden_blocks(saved):
    d = lax.axis_index("dp")
    blk = saved.shape[1] // 4
    flipped = saved.T
    near = lax.ppermute(rows(flipped, jnp.where(d == 0, blk, 2 * blk), blk), "dp", [(0, 1), (3, 2)])
    far = lax.ppermute(rows(flipped, jnp.where(d == 0, 2 * blk, 0), 2 * blk), "dp", [(0, 2), (3, 1)])
    mid = lax.ppermute(rows(flipped, jnp.where(d == 1, 2 * blk, 0), 2 * blk), "dp", [(1, 2), (2, 1)])
    return flipped, near, far, mid


def line_weight_grad(blocks, scaled, chunks):
    flipped, near, far, mid = blocks
    d = lax.axis_index("dp")
    blk = flipped.shape[0] // 4
    own_at = jnp.where(d == 1, blk, 0)
    end_at = jnp.where(d == 1, 0, blk)
    own = [rows(flipped, d * blk, blk), near, rows(mid, own_at, blk), rows(far, own_at, blk)]
    end = [rows(flipped, jnp.where(d == 1, 0, 3 * blk), blk), rows(mid, end_at, blk), rows(far, end_at, blk)]
    edge = (d == 0) | (d == 3)
    width = scaled.shape[1] // chunks
    pieces = []
    for c in range(chunks):
        sc = scaled[:, c * width:(c + 1) * width]
        inner = lax.ppermute(sc, "dp", [(0, 1), (3, 2)])
        across = lax.ppermute(sc, "dp", [(1, 2), (2, 1)])
        beyond = lax.ppermute(sc, "dp", [(0, 2), (3, 1)])
        mine = sum(
            jnp.dot(h, s, preferred_element_type=jnp.float32)
            for h, s in zip(own, [sc, inner, across, beyond])
        )
        theirs = sum(
            jnp.dot(h, s, preferred_element_type=jnp.float32)
            for h, s in zip(end, [sc, across, beyond])
        )
        tail = lax.ppermute(theirs.astype(jnp.bfloat16), "dp", [(1, 0), (2, 3)])
        pieces.append(mine + jnp.where(edge, tail.astype(jnp.float32), 0.0))
    return jnp.concatenate(pieces, axis=1), tail


def shards(grad_out, routes, gates, hidden, w_down):
    incoming = shifted(grad_out, "section", -1)[0]
    groups = lax.axis_size("expert")
    saved = hidden[0, 0, 0]
    weight = w_down[0, 0]
    slot_count = saved.shape[0]
    width = slot_count // groups
    model_width = incoming.shape[1]
    target = dispatch_targets(routes[0], groups, width)
    outgoing = dispatch_rows(incoming, gates[0], target, groups, width)
    line = lax.axis_size("dp") == 4 and saved.shape[1] % 4 == 0
    if line:
        blocks = hidden_blocks(saved)
        outgoing, blocks = lax.optimization_barrier((outgoing, blocks))
    piece = lax.all_to_all(outgoing, "expert", split_axis=0, concat_axis=0, tiled=True)
    scaled = piece.reshape(slot_count, model_width)
    if line:
        weight_grad, anchor = line_weight_grad(blocks, scaled, 4)
        late, _ = lax.optimization_barrier((scaled, anchor))
    else:
        full = lax.dot_general(
            saved, scaled, (((0,), (0,)), ((), ())), preferred_element_type=jnp.float32
        )
        weight_grad = lax.psum_scatter(
            full.astype(jnp.bfloat16), "dp", scatter_dimension=0, tiled=True
        ).astype(jnp.float32)
        late = scaled
    grad_rows_out = jnp.einsum(
        "sd,hd->sh", late, weight, preferred_element_type=jnp.float32
    ).astype(jnp.bfloat16)
    grad_hidden = grad_rows_out.reshape(1, 1, 1, slot_count, saved.shape[1])
    return (grad_hidden, weight_grad.reshape(1, 1, weight_grad.shape[0], model_width))


def solution(mesh):
    placed = (
        P("section", ("dp", "expert"), None),
        P("section", ("dp", "expert"), None),
        P("section", ("dp", "expert"), None),
        P("section", "dp", "expert", None, None),
        P("section", "expert", None, None),
    )
    return jax.shard_map(
        shards,
        mesh=mesh,
        in_specs=placed,
        out_specs=(P("section", "dp", "expert", None, None), P("section", "expert", "dp", None)),
        check_vma=False,
    )
```

```python
import jax
import jax.numpy as jnp
from jax import lax
from jax.sharding import PartitionSpec as P


def shifted(value, axis, steps):
    count = lax.axis_size(axis)
    pairs = [(source, (source + steps) % count) for source in range(count)]
    return lax.ppermute(value, axis, pairs)


def dispatch_targets(ids, count, width):
    flat_ids = ids.reshape(-1)
    onehot = (flat_ids[:, None] == jnp.arange(count, dtype=jnp.int32)[None, :]).astype(jnp.int32)
    position = jnp.sum((jnp.cumsum(onehot, axis=0) - 1) * onehot, axis=1)
    return (flat_ids * width + position).reshape(ids.shape)


def dispatch_rows(rows, weights, target, count, width):
    slots = count * width
    total = None
    for k in range(target.shape[1]):
        scaled = (weights[:, k:k + 1] * rows.astype(jnp.float32)).astype(jnp.bfloat16)
        onehot = lax.broadcasted_iota(jnp.int32, (slots, rows.shape[0]), 0) == target[None, :, k]
        term = jnp.dot(onehot.astype(jnp.bfloat16), scaled, preferred_element_type=jnp.float32)
        total = term if total is None else total + term
    return total.astype(jnp.bfloat16).reshape(count, width, rows.shape[1])


def send_hidden(saved):
    d = lax.axis_index("dp")
    blk = saved.shape[1] // 4
    column_block = lax.broadcasted_iota(jnp.int32, saved.shape, 1) // blk
    hsend = jnp.where(column_block == d, jnp.zeros_like(saved), saved)
    return lax.ppermute(hsend, "dp", [(0, 1), (3, 2)])


def line_weight_grad(saved, hfull, scaled, chunks):
    d = lax.axis_index("dp")
    hid = saved.shape[1]
    blk = hid // 4
    model_width = scaled.shape[1]
    unit = model_width // (2 * chunks)
    widths = [unit, 3 * unit, 3 * unit, model_width - 7 * unit] if chunks == 4 else [model_width]
    ends = [(0, 1), (3, 2)]
    lhs = jnp.concatenate([saved, hfull], axis=0)
    row2 = jnp.where(d == 1, 2 * blk, 0)
    row3a = jnp.where(d == 1, 0, 3 * blk)
    row3b = jnp.where(d == 1, 0, blk)
    own = d * blk
    half = jnp.where(d == 1, blk, 0)
    edge = (d == 0) | (d == 3)
    pieces = []
    begin = 0
    for width in widths:
        sc = scaled[:, begin:begin + width]
        begin += width
        srecv = lax.ppermute(sc, "dp", ends)
        rhs = jnp.concatenate([sc, srecv], axis=0)
        acc = lax.dot_general(
            lhs, rhs, (((0,), (0,)), ((), ())), preferred_element_type=jnp.float32
        )
        s2 = lax.dynamic_slice_in_dim(acc, row2, 2 * blk, axis=0).astype(jnp.bfloat16)
        r2 = lax.ppermute(s2, "dp", [(1, 2), (2, 1)])
        s3 = (
            lax.dynamic_slice_in_dim(acc, row3a, blk, axis=0)
            + lax.dynamic_slice_in_dim(r2, row3b, blk, axis=0).astype(jnp.float32)
        ).astype(jnp.bfloat16)
        r3 = lax.ppermute(s3, "dp", [(1, 0), (2, 3)])
        extra = jnp.where(edge, r3, lax.dynamic_slice_in_dim(r2, half, blk, axis=0))
        pieces.append(
            lax.dynamic_slice_in_dim(acc, own, blk, axis=0) + extra.astype(jnp.float32)
        )
    return jnp.concatenate(pieces, axis=1), s2


def shards(grad_out, routes, gates, hidden, w_down):
    incoming = shifted(grad_out, "section", -1)[0]
    groups = lax.axis_size("expert")
    saved = hidden[0, 0, 0]
    weight = w_down[0, 0]
    slot_count = saved.shape[0]
    width = slot_count // groups
    model_width = incoming.shape[1]
    target = dispatch_targets(routes[0], groups, width)
    outgoing = dispatch_rows(incoming, gates[0], target, groups, width)
    line = lax.axis_size("dp") == 4 and saved.shape[1] % 4 == 0
    if line:
        hfull = send_hidden(saved)
    piece = lax.all_to_all(outgoing, "expert", split_axis=0, concat_axis=0, tiled=True)
    scaled = piece.reshape(slot_count, model_width)
    if line:
        weight_grad, anchor = line_weight_grad(saved, hfull, scaled, 4)
        late, _ = lax.optimization_barrier((scaled, anchor))
    else:
        full = lax.dot_general(
            saved, scaled, (((0,), (0,)), ((), ())), preferred_element_type=jnp.float32
        )
        weight_grad = lax.psum_scatter(
            full.astype(jnp.bfloat16), "dp", scatter_dimension=0, tiled=True
        ).astype(jnp.float32)
        late = scaled
    grad_rows_out = jnp.einsum(
        "sd,hd->sh", late, weight, preferred_element_type=jnp.float32
    ).astype(jnp.bfloat16)
    grad_hidden = grad_rows_out.reshape(1, 1, 1, slot_count, saved.shape[1])
    return (grad_hidden, weight_grad.reshape(1, 1, weight_grad.shape[0], model_width))


def solution(mesh):
    placed = (
        P("section", ("dp", "expert"), None),
        P("section", ("dp", "expert"), None),
        P("section", ("dp", "expert"), None),
        P("section", "dp", "expert", None, None),
        P("section", "expert", None, None),
    )
    return jax.shard_map(
        shards,
        mesh=mesh,
        in_specs=placed,
        out_specs=(P("section", "dp", "expert", None, None), P("section", "expert", "dp", None)),
        check_vma=False,
    )
```

```python
import jax
import jax.numpy as jnp
from jax import lax
from jax.sharding import PartitionSpec as P


def shifted(value, axis, steps):
    count = lax.axis_size(axis)
    pairs = [(source, (source + steps) % count) for source in range(count)]
    return lax.ppermute(value, axis, pairs)


def dispatch_targets(ids, count, width):
    flat_ids = ids.reshape(-1)
    onehot = (flat_ids[:, None] == jnp.arange(count, dtype=jnp.int32)[None, :]).astype(jnp.int32)
    position = jnp.sum((jnp.cumsum(onehot, axis=0) - 1) * onehot, axis=1)
    return (flat_ids * width + position).reshape(ids.shape)


def dispatch_rows(rows, weights, target, count, width):
    slots = count * width
    total = None
    for k in range(target.shape[1]):
        scaled = (weights[:, k:k + 1] * rows.astype(jnp.float32)).astype(jnp.bfloat16)
        onehot = lax.broadcasted_iota(jnp.int32, (slots, rows.shape[0]), 0) == target[None, :, k]
        term = jnp.dot(onehot.astype(jnp.bfloat16), scaled, preferred_element_type=jnp.float32)
        total = term if total is None else total + term
    return total.astype(jnp.bfloat16).reshape(count, width, rows.shape[1])


def send_hidden(saved):
    d = lax.axis_index("dp")
    blk = saved.shape[1] // 4
    part = lax.dynamic_slice_in_dim(saved.T, jnp.where(d == 0, blk, 0), 3 * blk, axis=0)
    return lax.ppermute(part, "dp", [(0, 1), (3, 2)])


def line_weight_grad(saved, hfull, scaled, chunks):
    d = lax.axis_index("dp")
    hid = saved.shape[1]
    blk = hid // 4
    width = scaled.shape[1] // chunks
    ends = [(0, 1), (3, 2)]
    place = jnp.where(d == 1, blk, 0)
    row2 = jnp.where(d == 1, 2 * blk, 0)
    row3a = jnp.where(d == 1, 0, 3 * blk)
    row3b = jnp.where(d == 1, 0, blk)
    own = d * blk
    half = jnp.where(d == 1, blk, 0)
    edge = (d == 0) | (d == 3)
    pieces = []
    for c in range(chunks):
        sc = scaled[:, c * width:(c + 1) * width]
        srecv = lax.ppermute(sc, "dp", ends)
        acc = lax.dot_general(
            saved, sc, (((0,), (0,)), ((), ())), preferred_element_type=jnp.float32
        )
        near = jnp.dot(hfull, srecv, preferred_element_type=jnp.float32)
        acc = acc + lax.dynamic_update_slice_in_dim(jnp.zeros_like(acc), near, place, axis=0)
        s2 = lax.dynamic_slice_in_dim(acc, row2, 2 * blk, axis=0).astype(jnp.bfloat16)
        r2 = lax.ppermute(s2, "dp", [(1, 2), (2, 1)])
        s3 = (
            lax.dynamic_slice_in_dim(acc, row3a, blk, axis=0)
            + lax.dynamic_slice_in_dim(r2, row3b, blk, axis=0).astype(jnp.float32)
        ).astype(jnp.bfloat16)
        r3 = lax.ppermute(s3, "dp", [(1, 0), (2, 3)])
        extra = jnp.where(edge, r3, lax.dynamic_slice_in_dim(r2, half, blk, axis=0))
        pieces.append(
            lax.dynamic_slice_in_dim(acc, own, blk, axis=0) + extra.astype(jnp.float32)
        )
    return jnp.concatenate(pieces, axis=1), s2


def shards(grad_out, routes, gates, hidden, w_down):
    incoming = shifted(grad_out, "section", -1)[0]
    groups = lax.axis_size("expert")
    saved = hidden[0, 0, 0]
    weight = w_down[0, 0]
    slot_count = saved.shape[0]
    width = slot_count // groups
    model_width = incoming.shape[1]
    target = dispatch_targets(routes[0], groups, width)
    outgoing = dispatch_rows(incoming, gates[0], target, groups, width)
    line = lax.axis_size("dp") == 4 and saved.shape[1] % 4 == 0
    if line:
        hfull = send_hidden(saved)
    piece = lax.all_to_all(outgoing, "expert", split_axis=0, concat_axis=0, tiled=True)
    scaled = piece.reshape(slot_count, model_width)
    if line:
        weight_grad, anchor = line_weight_grad(saved, hfull, scaled, 4)
        late, _ = lax.optimization_barrier((scaled, anchor))
    else:
        full = lax.dot_general(
            saved, scaled, (((0,), (0,)), ((), ())), preferred_element_type=jnp.float32
        )
        weight_grad = lax.psum_scatter(
            full.astype(jnp.bfloat16), "dp", scatter_dimension=0, tiled=True
        ).astype(jnp.float32)
        late = scaled
    grad_rows_out = jnp.einsum(
        "sd,hd->sh", late, weight, preferred_element_type=jnp.float32
    ).astype(jnp.bfloat16)
    grad_hidden = grad_rows_out.reshape(1, 1, 1, slot_count, saved.shape[1])
    return (grad_hidden, weight_grad.reshape(1, 1, weight_grad.shape[0], model_width))


def solution(mesh):
    placed = (
        P("section", ("dp", "expert"), None),
        P("section", ("dp", "expert"), None),
        P("section", ("dp", "expert"), None),
        P("section", "dp", "expert", None, None),
        P("section", "expert", None, None),
    )
    return jax.shard_map(
        shards,
        mesh=mesh,
        in_specs=placed,
        out_specs=(P("section", "dp", "expert", None, None), P("section", "expert", "dp", None)),
        check_vma=False,
    )
```

```python
import jax
import jax.numpy as jnp
from jax import lax
from jax.sharding import PartitionSpec as P


def shifted(value, axis, steps):
    count = lax.axis_size(axis)
    pairs = [(source, (source + steps) % count) for source in range(count)]
    return lax.ppermute(value, axis, pairs)


def dispatch_targets(ids, count, width):
    flat_ids = ids.reshape(-1)
    onehot = (flat_ids[:, None] == jnp.arange(count, dtype=jnp.int32)[None, :]).astype(jnp.int32)
    position = jnp.sum((jnp.cumsum(onehot, axis=0) - 1) * onehot, axis=1)
    return (flat_ids * width + position).reshape(ids.shape)


def dispatch_rows(rows, weights, target, count, width):
    slots = count * width
    total = None
    for k in range(target.shape[1]):
        scaled = (weights[:, k:k + 1] * rows.astype(jnp.float32)).astype(jnp.bfloat16)
        onehot = lax.broadcasted_iota(jnp.int32, (slots, rows.shape[0]), 0) == target[None, :, k]
        term = jnp.dot(onehot.astype(jnp.bfloat16), scaled, preferred_element_type=jnp.float32)
        total = term if total is None else total + term
    return total.astype(jnp.bfloat16).reshape(count, width, rows.shape[1])


def send_hidden(saved):
    d = lax.axis_index("dp")
    blk = saved.shape[1] // 4
    column_block = lax.broadcasted_iota(jnp.int32, saved.shape, 1) // blk
    hsend = jnp.where(column_block == d, jnp.zeros_like(saved), saved)
    return lax.ppermute(hsend, "dp", [(0, 1), (3, 2)])


def line_weight_grad(saved, hfull, scaled, chunks):
    d = lax.axis_index("dp")
    hid = saved.shape[1]
    blk = hid // 4
    width = scaled.shape[1] // chunks
    ends = [(0, 1), (3, 2)]
    lhs = jnp.concatenate([saved, hfull], axis=0)
    row2 = jnp.where(d == 1, 2 * blk, 0)
    row3a = jnp.where(d == 1, 0, 3 * blk)
    row3b = jnp.where(d == 1, 0, blk)
    own = d * blk
    half = jnp.where(d == 1, blk, 0)
    edge = (d == 0) | (d == 3)
    pieces = []
    for c in range(chunks):
        sc = scaled[:, c * width:(c + 1) * width]
        srecv = lax.ppermute(sc, "dp", ends)
        rhs = jnp.concatenate([sc, srecv], axis=0)
        acc = lax.dot_general(
            lhs, rhs, (((0,), (0,)), ((), ())), preferred_element_type=jnp.float32
        )
        s2 = lax.dynamic_slice_in_dim(acc, row2, 2 * blk, axis=0).astype(jnp.bfloat16)
        r2 = lax.ppermute(s2, "dp", [(1, 2), (2, 1)])
        s3 = (
            lax.dynamic_slice_in_dim(acc, row3a, blk, axis=0)
            + lax.dynamic_slice_in_dim(r2, row3b, blk, axis=0).astype(jnp.float32)
        ).astype(jnp.bfloat16)
        r3 = lax.ppermute(s3, "dp", [(1, 0), (2, 3)])
        extra = jnp.where(edge, r3, lax.dynamic_slice_in_dim(r2, half, blk, axis=0))
        pieces.append(
            lax.dynamic_slice_in_dim(acc, own, blk, axis=0) + extra.astype(jnp.float32)
        )
    return jnp.concatenate(pieces, axis=1), s2


def shards(grad_out, routes, gates, hidden, w_down):
    groups = lax.axis_size("expert")
    saved = hidden[0, 0, 0]
    weight = w_down[0, 0]
    slot_count = saved.shape[0]
    width = slot_count // groups
    model_width = grad_out.shape[2]
    target = dispatch_targets(routes[0], groups, width)
    line = lax.axis_size("dp") == 4 and saved.shape[1] % 4 == 0
    if line:
        hfull = send_hidden(saved)
    halves = 2 if model_width % 256 == 0 else 1
    step = model_width // halves
    parts = []
    for h in range(halves):
        rows = shifted(grad_out[0, :, h * step:(h + 1) * step], "section", -1)
        outgoing = dispatch_rows(rows, gates[0], target, groups, width)
        piece = lax.all_to_all(outgoing, "expert", split_axis=0, concat_axis=0, tiled=True)
        parts.append(piece.reshape(slot_count, step))
    scaled = jnp.concatenate(parts, axis=1)
    if line:
        weight_grad, anchor = line_weight_grad(saved, hfull, scaled, 4)
        late, _ = lax.optimization_barrier((scaled, anchor))
    else:
        full = lax.dot_general(
            saved, scaled, (((0,), (0,)), ((), ())), preferred_element_type=jnp.float32
        )
        weight_grad = lax.psum_scatter(
            full.astype(jnp.bfloat16), "dp", scatter_dimension=0, tiled=True
        ).astype(jnp.float32)
        late = scaled
    grad_rows_out = jnp.einsum(
        "sd,hd->sh", late, weight, preferred_element_type=jnp.float32
    ).astype(jnp.bfloat16)
    grad_hidden = grad_rows_out.reshape(1, 1, 1, slot_count, saved.shape[1])
    return (grad_hidden, weight_grad.reshape(1, 1, weight_grad.shape[0], model_width))


def solution(mesh):
    placed = (
        P("section", ("dp", "expert"), None),
        P("section", ("dp", "expert"), None),
        P("section", ("dp", "expert"), None),
        P("section", "dp", "expert", None, None),
        P("section", "expert", None, None),
    )
    return jax.shard_map(
        shards,
        mesh=mesh,
        in_specs=placed,
        out_specs=(P("section", "dp", "expert", None, None), P("section", "expert", "dp", None)),
        check_vma=False,
    )
```

```python
import jax
import jax.numpy as jnp
from jax import lax
from jax.sharding import PartitionSpec as P


def shifted(value, axis, steps):
    count = lax.axis_size(axis)
    pairs = [(source, (source + steps) % count) for source in range(count)]
    return lax.ppermute(value, axis, pairs)


def dispatch_targets(ids, count, width):
    flat_ids = ids.reshape(-1)
    onehot = (flat_ids[:, None] == jnp.arange(count, dtype=jnp.int32)[None, :]).astype(jnp.int32)
    position = jnp.sum((jnp.cumsum(onehot, axis=0) - 1) * onehot, axis=1)
    return (flat_ids * width + position).reshape(ids.shape)


def dispatch_rows(rows, weights, target, count, width):
    slots = count * width
    total = None
    for k in range(target.shape[1]):
        scaled = (weights[:, k:k + 1] * rows.astype(jnp.float32)).astype(jnp.bfloat16)
        onehot = lax.broadcasted_iota(jnp.int32, (slots, rows.shape[0]), 0) == target[None, :, k]
        term = jnp.dot(onehot.astype(jnp.bfloat16), scaled, preferred_element_type=jnp.float32)
        total = term if total is None else total + term
    return total.astype(jnp.bfloat16).reshape(count, width, rows.shape[1])


def send_hidden(saved):
    d = lax.axis_index("dp")
    blk = saved.shape[1] // 4
    column_block = lax.broadcasted_iota(jnp.int32, saved.shape, 1) // blk
    hsend = jnp.where(column_block == d, jnp.zeros_like(saved), saved)
    return lax.ppermute(hsend, "dp", [(0, 1), (3, 2)])


def line_weight_grad(saved, hfull, scaled, chunks):
    d = lax.axis_index("dp")
    hid = saved.shape[1]
    blk = hid // 4
    width = scaled.shape[1] // chunks
    ends = [(0, 1), (3, 2)]
    lhs = jnp.concatenate([saved, hfull], axis=0)
    row2 = jnp.where(d == 1, 2 * blk, 0)
    row3a = jnp.where(d == 1, 0, 3 * blk)
    row3b = jnp.where(d == 1, 0, blk)
    own = d * blk
    half = jnp.where(d == 1, blk, 0)
    edge = (d == 0) | (d == 3)
    result = jnp.zeros((blk, scaled.shape[1]), jnp.float32)
    for c in range(chunks):
        sc = scaled[:, c * width:(c + 1) * width]
        srecv = lax.ppermute(sc, "dp", ends)
        rhs = jnp.concatenate([sc, srecv], axis=0)
        acc = lax.dot_general(
            lhs, rhs, (((0,), (0,)), ((), ())), preferred_element_type=jnp.float32
        )
        s2 = lax.dynamic_slice_in_dim(acc, row2, 2 * blk, axis=0).astype(jnp.bfloat16)
        r2 = lax.ppermute(s2, "dp", [(1, 2), (2, 1)])
        s3 = (
            lax.dynamic_slice_in_dim(acc, row3a, blk, axis=0)
            + lax.dynamic_slice_in_dim(r2, row3b, blk, axis=0).astype(jnp.float32)
        ).astype(jnp.bfloat16)
        r3 = lax.ppermute(s3, "dp", [(1, 0), (2, 3)])
        extra = jnp.where(edge, r3, lax.dynamic_slice_in_dim(r2, half, blk, axis=0))
        result = lax.dynamic_update_slice_in_dim(
            result, lax.dynamic_slice_in_dim(acc, own, blk, axis=0) + extra.astype(jnp.float32),
            c * width, axis=1,
        )
    return result, s2


def shards(grad_out, routes, gates, hidden, w_down):
    incoming = shifted(grad_out, "section", -1)[0]
    groups = lax.axis_size("expert")
    saved = hidden[0, 0, 0]
    weight = w_down[0, 0]
    slot_count = saved.shape[0]
    width = slot_count // groups
    model_width = incoming.shape[1]
    target = dispatch_targets(routes[0], groups, width)
    outgoing = dispatch_rows(incoming, gates[0], target, groups, width)
    line = lax.axis_size("dp") == 4 and saved.shape[1] % 4 == 0
    if line:
        hfull = send_hidden(saved)
    piece = lax.all_to_all(outgoing, "expert", split_axis=0, concat_axis=0, tiled=True)
    scaled = piece.reshape(slot_count, model_width)
    if line:
        weight_grad, anchor = line_weight_grad(saved, hfull, scaled, 4)
        late, _ = lax.optimization_barrier((scaled, anchor))
    else:
        full = lax.dot_general(
            saved, scaled, (((0,), (0,)), ((), ())), preferred_element_type=jnp.float32
        )
        weight_grad = lax.psum_scatter(
            full.astype(jnp.bfloat16), "dp", scatter_dimension=0, tiled=True
        ).astype(jnp.float32)
        late = scaled
    grad_rows_out = jnp.einsum(
        "sd,hd->sh", late, weight, preferred_element_type=jnp.float32
    ).astype(jnp.bfloat16)
    grad_hidden = grad_rows_out.reshape(1, 1, 1, slot_count, saved.shape[1])
    return (grad_hidden, weight_grad.reshape(1, 1, weight_grad.shape[0], model_width))


def solution(mesh):
    placed = (
        P("section", ("dp", "expert"), None),
        P("section", ("dp", "expert"), None),
        P("section", ("dp", "expert"), None),
        P("section", "dp", "expert", None, None),
        P("section", "expert", None, None),
    )
    return jax.shard_map(
        shards,
        mesh=mesh,
        in_specs=placed,
        out_specs=(P("section", "dp", "expert", None, None), P("section", "expert", "dp", None)),
        check_vma=False,
    )
```

```python
import jax
import jax.numpy as jnp
from jax import lax
from jax.sharding import PartitionSpec as P


def shifted(value, axis, steps):
    count = lax.axis_size(axis)
    pairs = [(source, (source + steps) % count) for source in range(count)]
    return lax.ppermute(value, axis, pairs)


def dispatch_targets(ids, count, width):
    flat_ids = ids.reshape(-1)
    onehot = (flat_ids[:, None] == jnp.arange(count, dtype=jnp.int32)[None, :]).astype(jnp.int32)
    position = jnp.sum((jnp.cumsum(onehot, axis=0) - 1) * onehot, axis=1)
    return (flat_ids * width + position).reshape(ids.shape)


def dispatch_rows(rows, weights, target, count, width):
    slots = count * width
    total = None
    for k in range(target.shape[1]):
        scaled = (weights[:, k:k + 1] * rows.astype(jnp.float32)).astype(jnp.bfloat16)
        onehot = lax.broadcasted_iota(jnp.int32, (slots, rows.shape[0]), 0) == target[None, :, k]
        term = jnp.dot(onehot.astype(jnp.bfloat16), scaled, preferred_element_type=jnp.float32)
        total = term if total is None else total + term
    return total.astype(jnp.bfloat16).reshape(count, width, rows.shape[1])


def send_hidden(saved):
    d = lax.axis_index("dp")
    blk = saved.shape[1] // 4
    column_block = lax.broadcasted_iota(jnp.int32, saved.shape, 1) // blk
    hsend = jnp.where(column_block == d, jnp.zeros_like(saved), saved)
    return lax.ppermute(hsend, "dp", [(0, 1), (3, 2)])


def line_weight_grad(saved, hfull, scaled, chunks):
    d = lax.axis_index("dp")
    hid = saved.shape[1]
    blk = hid // 4
    width = scaled.shape[1] // chunks
    ends = [(0, 1), (3, 2)]
    lhs = jnp.concatenate([saved, hfull], axis=0)
    row2 = jnp.where(d == 1, 2 * blk, 0)
    row3a = jnp.where(d == 1, 0, 3 * blk)
    row3b = jnp.where(d == 1, 0, blk)
    own = d * blk
    half = jnp.where(d == 1, blk, 0)
    edge = (d == 0) | (d == 3)
    pieces = []
    for c in range(chunks):
        sc = scaled[:, c * width:(c + 1) * width]
        srecv = lax.ppermute(sc, "dp", ends)
        rhs = jnp.concatenate([sc, srecv], axis=0)
        acc = lax.dot_general(
            lhs, rhs, (((0,), (0,)), ((), ())), preferred_element_type=jnp.float32
        )
        s2 = lax.dynamic_slice_in_dim(acc, row2, 2 * blk, axis=0).astype(jnp.bfloat16)
        r2 = lax.ppermute(s2, "dp", [(1, 2), (2, 1)])
        s3 = (
            lax.dynamic_slice_in_dim(acc, row3a, blk, axis=0)
            + lax.dynamic_slice_in_dim(r2, row3b, blk, axis=0).astype(jnp.float32)
        ).astype(jnp.bfloat16)
        r3 = lax.ppermute(s3, "dp", [(1, 0), (2, 3)])
        extra = jnp.where(edge, r3, lax.dynamic_slice_in_dim(r2, half, blk, axis=0))
        pieces.append(
            lax.dynamic_slice_in_dim(acc, own, blk, axis=0) + extra.astype(jnp.float32)
        )
    return jnp.concatenate(pieces, axis=1), s2


def shards(grad_out, routes, gates, hidden, w_down):
    incoming = shifted(grad_out, "section", -1)[0]
    groups = lax.axis_size("expert")
    saved = hidden[0, 0, 0]
    weight = w_down[0, 0]
    slot_count = saved.shape[0]
    width = slot_count // groups
    model_width = incoming.shape[1]
    target = dispatch_targets(routes[0], groups, width)
    outgoing = dispatch_rows(incoming, gates[0], target, groups, width)
    line = lax.axis_size("dp") == 4 and saved.shape[1] % 4 == 0
    if line:
        hfull = send_hidden(saved)
    piece = lax.all_to_all(outgoing, "expert", split_axis=0, concat_axis=0, tiled=True)
    scaled = piece.reshape(slot_count, model_width)
    if line:
        weight_grad, anchor = line_weight_grad(saved, hfull, scaled, 2)
        late, _ = lax.optimization_barrier((scaled, anchor))
    else:
        full = lax.dot_general(
            saved, scaled, (((0,), (0,)), ((), ())), preferred_element_type=jnp.float32
        )
        weight_grad = lax.psum_scatter(
            full.astype(jnp.bfloat16), "dp", scatter_dimension=0, tiled=True
        ).astype(jnp.float32)
        late = scaled
    grad_rows_out = jnp.einsum(
        "sd,hd->sh", late, weight, preferred_element_type=jnp.float32
    ).astype(jnp.bfloat16)
    grad_hidden = grad_rows_out.reshape(1, 1, 1, slot_count, saved.shape[1])
    return (grad_hidden, weight_grad.reshape(1, 1, weight_grad.shape[0], model_width))


def solution(mesh):
    placed = (
        P("section", ("dp", "expert"), None),
        P("section", ("dp", "expert"), None),
        P("section", ("dp", "expert"), None),
        P("section", "dp", "expert", None, None),
        P("section", "expert", None, None),
    )
    return jax.shard_map(
        shards,
        mesh=mesh,
        in_specs=placed,
        out_specs=(P("section", "dp", "expert", None, None), P("section", "expert", "dp", None)),
        check_vma=False,
    )
```

```python
import jax
import jax.numpy as jnp
from jax import lax
from jax.sharding import PartitionSpec as P


def shifted(value, axis, steps):
    count = lax.axis_size(axis)
    pairs = [(source, (source + steps) % count) for source in range(count)]
    return lax.ppermute(value, axis, pairs)


def dispatch_targets(ids, count, width):
    flat_ids = ids.reshape(-1)
    onehot = (flat_ids[:, None] == jnp.arange(count, dtype=jnp.int32)[None, :]).astype(jnp.int32)
    position = jnp.sum((jnp.cumsum(onehot, axis=0) - 1) * onehot, axis=1)
    return (flat_ids * width + position).reshape(ids.shape)


def dispatch_rows(rows, weights, target, count, width):
    slots = count * width
    total = None
    for k in range(target.shape[1]):
        scaled = (weights[:, k:k + 1] * rows.astype(jnp.float32)).astype(jnp.bfloat16)
        onehot = lax.broadcasted_iota(jnp.int32, (slots, rows.shape[0]), 0) == target[None, :, k]
        term = jnp.dot(onehot.astype(jnp.bfloat16), scaled, preferred_element_type=jnp.float32)
        total = term if total is None else total + term
    return total.astype(jnp.bfloat16).reshape(count, width, rows.shape[1])


def send_hidden(saved):
    d = lax.axis_index("dp")
    blk = saved.shape[1] // 4
    column_block = lax.broadcasted_iota(jnp.int32, saved.shape, 1) // blk
    hsend = jnp.where(column_block == d, jnp.zeros_like(saved), saved)
    return lax.ppermute(hsend, "dp", [(0, 1), (3, 2)])


def line_weight_grad(saved, hfull, scaled, chunks):
    d = lax.axis_index("dp")
    hid = saved.shape[1]
    blk = hid // 4
    width = scaled.shape[1] // chunks
    ends = [(0, 1), (3, 2)]
    lhs = jnp.concatenate([saved, hfull], axis=0)
    row2 = jnp.where(d == 1, 2 * blk, 0)
    row3a = jnp.where(d == 1, 0, 3 * blk)
    row3b = jnp.where(d == 1, 0, blk)
    own = d * blk
    half = jnp.where(d == 1, blk, 0)
    edge = (d == 0) | (d == 3)
    pieces = []
    for c in range(chunks):
        sc = scaled[:, c * width:(c + 1) * width]
        srecv = lax.ppermute(sc, "dp", ends)
        rhs = jnp.concatenate([sc, srecv], axis=0)
        acc = lax.dot_general(
            lhs, rhs, (((0,), (0,)), ((), ())), preferred_element_type=jnp.float32
        )
        s2 = lax.dynamic_slice_in_dim(acc, row2, 2 * blk, axis=0).astype(jnp.bfloat16)
        r2 = lax.ppermute(s2, "dp", [(1, 2), (2, 1)])
        s3 = (
            lax.dynamic_slice_in_dim(acc, row3a, blk, axis=0)
            + lax.dynamic_slice_in_dim(r2, row3b, blk, axis=0).astype(jnp.float32)
        ).astype(jnp.bfloat16)
        r3 = lax.ppermute(s3, "dp", [(1, 0), (2, 3)])
        extra = jnp.where(edge, r3, lax.dynamic_slice_in_dim(r2, half, blk, axis=0))
        pieces.append(
            lax.dynamic_slice_in_dim(acc, own, blk, axis=0) + extra.astype(jnp.float32)
        )
    return jnp.concatenate(pieces, axis=1), s2


def shards(grad_out, routes, gates, hidden, w_down):
    incoming = shifted(grad_out, "section", -1)[0]
    groups = lax.axis_size("expert")
    saved = hidden[0, 0, 0]
    weight = w_down[0, 0]
    slot_count = saved.shape[0]
    width = slot_count // groups
    model_width = incoming.shape[1]
    target = dispatch_targets(routes[0], groups, width)
    outgoing = dispatch_rows(incoming, gates[0], target, groups, width)
    line = lax.axis_size("dp") == 4 and saved.shape[1] % 4 == 0
    if line:
        hfull = send_hidden(saved)
    piece = lax.all_to_all(outgoing, "expert", split_axis=0, concat_axis=0, tiled=True)
    scaled = piece.reshape(slot_count, model_width)
    if line:
        weight_grad, anchor = line_weight_grad(saved, hfull, scaled, 4)
        late = scaled
    else:
        full = lax.dot_general(
            saved, scaled, (((0,), (0,)), ((), ())), preferred_element_type=jnp.float32
        )
        weight_grad = lax.psum_scatter(
            full.astype(jnp.bfloat16), "dp", scatter_dimension=0, tiled=True
        ).astype(jnp.float32)
        late = scaled
    grad_rows_out = jnp.einsum(
        "sd,hd->sh", late, weight, preferred_element_type=jnp.float32
    ).astype(jnp.bfloat16)
    grad_hidden = grad_rows_out.reshape(1, 1, 1, slot_count, saved.shape[1])
    return (grad_hidden, weight_grad.reshape(1, 1, weight_grad.shape[0], model_width))


def solution(mesh):
    placed = (
        P("section", ("dp", "expert"), None),
        P("section", ("dp", "expert"), None),
        P("section", ("dp", "expert"), None),
        P("section", "dp", "expert", None, None),
        P("section", "expert", None, None),
    )
    return jax.shard_map(
        shards,
        mesh=mesh,
        in_specs=placed,
        out_specs=(P("section", "dp", "expert", None, None), P("section", "expert", "dp", None)),
        check_vma=False,
    )
```

```python
import jax
import jax.numpy as jnp
from jax import lax
from jax.sharding import PartitionSpec as P


def shifted(value, axis, steps):
    count = lax.axis_size(axis)
    pairs = [(source, (source + steps) % count) for source in range(count)]
    return lax.ppermute(value, axis, pairs)


def dispatch_targets(ids, count, width):
    flat_ids = ids.reshape(-1)
    onehot = (flat_ids[:, None] == jnp.arange(count, dtype=jnp.int32)[None, :]).astype(jnp.int32)
    position = jnp.sum((jnp.cumsum(onehot, axis=0) - 1) * onehot, axis=1)
    return (flat_ids * width + position).reshape(ids.shape)


def dispatch_rows(rows, weights, target, count, width):
    slots = count * width
    total = None
    for k in range(target.shape[1]):
        scaled = (weights[:, k:k + 1] * rows.astype(jnp.float32)).astype(jnp.bfloat16)
        onehot = lax.broadcasted_iota(jnp.int32, (slots, rows.shape[0]), 0) == target[None, :, k]
        term = jnp.dot(onehot.astype(jnp.bfloat16), scaled, preferred_element_type=jnp.float32)
        total = term if total is None else total + term
    return total.astype(jnp.bfloat16).reshape(count, width, rows.shape[1])


def send_hidden(saved):
    return lax.ppermute(saved, "dp", [(0, 1), (3, 2)])


def line_weight_grad(saved, hfull, scaled, chunks):
    d = lax.axis_index("dp")
    hid = saved.shape[1]
    blk = hid // 4
    width = scaled.shape[1] // chunks
    ends = [(0, 1), (3, 2)]
    lhs = jnp.concatenate([saved, hfull], axis=0)
    row2 = jnp.where(d == 1, 2 * blk, 0)
    row3a = jnp.where(d == 1, 0, 3 * blk)
    row3b = jnp.where(d == 1, 0, blk)
    own = d * blk
    half = jnp.where(d == 1, blk, 0)
    edge = (d == 0) | (d == 3)
    pieces = []
    for c in range(chunks):
        sc = scaled[:, c * width:(c + 1) * width]
        srecv = lax.ppermute(sc, "dp", ends)
        rhs = jnp.concatenate([sc, srecv], axis=0)
        acc = lax.dot_general(
            lhs, rhs, (((0,), (0,)), ((), ())), preferred_element_type=jnp.float32
        )
        s2 = lax.dynamic_slice_in_dim(acc, row2, 2 * blk, axis=0).astype(jnp.bfloat16)
        r2 = lax.ppermute(s2, "dp", [(1, 2), (2, 1)])
        s3 = (
            lax.dynamic_slice_in_dim(acc, row3a, blk, axis=0)
            + lax.dynamic_slice_in_dim(r2, row3b, blk, axis=0).astype(jnp.float32)
        ).astype(jnp.bfloat16)
        r3 = lax.ppermute(s3, "dp", [(1, 0), (2, 3)])
        inside = lax.dynamic_slice_in_dim(acc, own, blk, axis=0) + lax.dynamic_slice_in_dim(
            r2, half, blk, axis=0
        ).astype(jnp.float32)
        pieces.append(jnp.where(edge, r3.astype(jnp.float32), inside))
    return jnp.concatenate(pieces, axis=1), s2


def shards(grad_out, routes, gates, hidden, w_down):
    incoming = shifted(grad_out, "section", -1)[0]
    groups = lax.axis_size("expert")
    saved = hidden[0, 0, 0]
    weight = w_down[0, 0]
    slot_count = saved.shape[0]
    width = slot_count // groups
    model_width = incoming.shape[1]
    target = dispatch_targets(routes[0], groups, width)
    outgoing = dispatch_rows(incoming, gates[0], target, groups, width)
    line = lax.axis_size("dp") == 4 and saved.shape[1] % 4 == 0
    if line:
        hfull = send_hidden(saved)
    piece = lax.all_to_all(outgoing, "expert", split_axis=0, concat_axis=0, tiled=True)
    scaled = piece.reshape(slot_count, model_width)
    if line:
        weight_grad, anchor = line_weight_grad(saved, hfull, scaled, 4)
        late = scaled
    else:
        full = lax.dot_general(
            saved, scaled, (((0,), (0,)), ((), ())), preferred_element_type=jnp.float32
        )
        weight_grad = lax.psum_scatter(
            full.astype(jnp.bfloat16), "dp", scatter_dimension=0, tiled=True
        ).astype(jnp.float32)
        late = scaled
    grad_rows_out = jnp.einsum(
        "sd,hd->sh", late, weight, preferred_element_type=jnp.float32
    ).astype(jnp.bfloat16)
    grad_hidden = grad_rows_out.reshape(1, 1, 1, slot_count, saved.shape[1])
    return (grad_hidden, weight_grad.reshape(1, 1, weight_grad.shape[0], model_width))


def solution(mesh):
    placed = (
        P("section", ("dp", "expert"), None),
        P("section", ("dp", "expert"), None),
        P("section", ("dp", "expert"), None),
        P("section", "dp", "expert", None, None),
        P("section", "expert", None, None),
    )
    return jax.shard_map(
        shards,
        mesh=mesh,
        in_specs=placed,
        out_specs=(P("section", "dp", "expert", None, None), P("section", "expert", "dp", None)),
        check_vma=False,
    )
```

```python
import jax
import jax.numpy as jnp
from jax import lax
from jax.sharding import PartitionSpec as P


def shifted(value, axis, steps):
    count = lax.axis_size(axis)
    pairs = [(source, (source + steps) % count) for source in range(count)]
    return lax.ppermute(value, axis, pairs)


def dispatch_targets(ids, count, width):
    flat_ids = ids.reshape(-1)
    onehot = (flat_ids[:, None] == jnp.arange(count, dtype=jnp.int32)[None, :]).astype(jnp.int32)
    position = jnp.sum((jnp.cumsum(onehot, axis=0) - 1) * onehot, axis=1)
    return (flat_ids * width + position).reshape(ids.shape)


def dispatch_rows(rows, weights, target, count, width):
    slots = count * width
    total = None
    for k in range(target.shape[1]):
        scaled = (weights[:, k:k + 1] * rows.astype(jnp.float32)).astype(jnp.bfloat16)
        onehot = lax.broadcasted_iota(jnp.int32, (slots, rows.shape[0]), 0) == target[None, :, k]
        term = jnp.dot(onehot.astype(jnp.bfloat16), scaled, preferred_element_type=jnp.float32)
        total = term if total is None else total + term
    return total.astype(jnp.bfloat16).reshape(count, width, rows.shape[1])


def send_hidden(saved):
    d = lax.axis_index("dp")
    blk = saved.shape[1] // 4
    column_block = lax.broadcasted_iota(jnp.int32, saved.shape, 1) // blk
    hsend = jnp.where(column_block == d, jnp.zeros_like(saved), saved)
    return lax.ppermute(hsend, "dp", [(0, 1), (3, 2)])


def line_weight_grad(saved, hfull, scaled, chunks):
    d = lax.axis_index("dp")
    hid = saved.shape[1]
    blk = hid // 4
    width = scaled.shape[1] // chunks
    ends = [(0, 1), (3, 2)]
    lhs = jnp.concatenate([saved, hfull], axis=0)
    row2 = jnp.where(d == 1, 2 * blk, 0)
    lhs2 = lax.dynamic_slice_in_dim(lhs, row2, 2 * blk, axis=1)
    row3a = jnp.where(d == 1, 0, 3 * blk)
    row3b = jnp.where(d == 1, 0, blk)
    own = d * blk
    half = jnp.where(d == 1, blk, 0)
    edge = (d == 0) | (d == 3)
    pieces = []
    for c in range(chunks):
        sc = scaled[:, c * width:(c + 1) * width]
        srecv = lax.ppermute(sc, "dp", ends)
        rhs = jnp.concatenate([sc, srecv], axis=0)
        acc = lax.dot_general(
            lhs, rhs, (((0,), (0,)), ((), ())), preferred_element_type=jnp.float32
        )
        s2 = lax.dot_general(
            lhs2, rhs, (((0,), (0,)), ((), ())), preferred_element_type=jnp.float32
        ).astype(jnp.bfloat16)
        r2 = lax.ppermute(s2, "dp", [(1, 2), (2, 1)])
        s3 = (
            lax.dynamic_slice_in_dim(acc, row3a, blk, axis=0)
            + lax.dynamic_slice_in_dim(r2, row3b, blk, axis=0).astype(jnp.float32)
        ).astype(jnp.bfloat16)
        r3 = lax.ppermute(s3, "dp", [(1, 0), (2, 3)])
        extra = jnp.where(edge, r3, lax.dynamic_slice_in_dim(r2, half, blk, axis=0))
        pieces.append(
            lax.dynamic_slice_in_dim(acc, own, blk, axis=0) + extra.astype(jnp.float32)
        )
    return jnp.concatenate(pieces, axis=1), s2


def shards(grad_out, routes, gates, hidden, w_down):
    incoming = shifted(grad_out, "section", -1)[0]
    groups = lax.axis_size("expert")
    saved = hidden[0, 0, 0]
    weight = w_down[0, 0]
    slot_count = saved.shape[0]
    width = slot_count // groups
    model_width = incoming.shape[1]
    target = dispatch_targets(routes[0], groups, width)
    outgoing = dispatch_rows(incoming, gates[0], target, groups, width)
    line = lax.axis_size("dp") == 4 and saved.shape[1] % 4 == 0
    if line:
        hfull = send_hidden(saved)
    piece = lax.all_to_all(outgoing, "expert", split_axis=0, concat_axis=0, tiled=True)
    scaled = piece.reshape(slot_count, model_width)
    if line:
        weight_grad, anchor = line_weight_grad(saved, hfull, scaled, 4)
        late = scaled
    else:
        full = lax.dot_general(
            saved, scaled, (((0,), (0,)), ((), ())), preferred_element_type=jnp.float32
        )
        weight_grad = lax.psum_scatter(
            full.astype(jnp.bfloat16), "dp", scatter_dimension=0, tiled=True
        ).astype(jnp.float32)
        late = scaled
    grad_rows_out = jnp.einsum(
        "sd,hd->sh", late, weight, preferred_element_type=jnp.float32
    ).astype(jnp.bfloat16)
    grad_hidden = grad_rows_out.reshape(1, 1, 1, slot_count, saved.shape[1])
    return (grad_hidden, weight_grad.reshape(1, 1, weight_grad.shape[0], model_width))


def solution(mesh):
    placed = (
        P("section", ("dp", "expert"), None),
        P("section", ("dp", "expert"), None),
        P("section", ("dp", "expert"), None),
        P("section", "dp", "expert", None, None),
        P("section", "expert", None, None),
    )
    return jax.shard_map(
        shards,
        mesh=mesh,
        in_specs=placed,
        out_specs=(P("section", "dp", "expert", None, None), P("section", "expert", "dp", None)),
        check_vma=False,
    )
```

```python
import jax
import jax.numpy as jnp
from jax import lax
from jax.sharding import PartitionSpec as P


def shifted(value, axis, steps):
    count = lax.axis_size(axis)
    pairs = [(source, (source + steps) % count) for source in range(count)]
    return lax.ppermute(value, axis, pairs)


def dispatch_targets(ids, count, width):
    flat_ids = ids.reshape(-1)
    onehot = (flat_ids[:, None] == jnp.arange(count, dtype=jnp.int32)[None, :]).astype(jnp.int32)
    position = jnp.sum((jnp.cumsum(onehot, axis=0) - 1) * onehot, axis=1)
    return (flat_ids * width + position).reshape(ids.shape)


def dispatch_rows(rows, weights, target, count, width):
    slots = count * width
    total = None
    for k in range(target.shape[1]):
        scaled = (weights[:, k:k + 1] * rows.astype(jnp.float32)).astype(jnp.bfloat16)
        onehot = lax.broadcasted_iota(jnp.int32, (slots, rows.shape[0]), 0) == target[None, :, k]
        term = jnp.dot(onehot.astype(jnp.bfloat16), scaled, preferred_element_type=jnp.float32)
        total = term if total is None else total + term
    return total.astype(jnp.bfloat16).reshape(count, width, rows.shape[1])


def send_hidden(saved):
    d = lax.axis_index("dp")
    blk = saved.shape[1] // 4
    column_block = lax.broadcasted_iota(jnp.int32, saved.shape, 1) // blk
    hsend = jnp.where(column_block == d, jnp.zeros_like(saved), saved)
    return lax.ppermute(hsend, "dp", [(0, 1), (3, 2)])


def line_weight_grad(saved, hfull, scaled, chunks):
    d = lax.axis_index("dp")
    hid = saved.shape[1]
    blk = hid // 4
    width = scaled.shape[1] // chunks
    ends = [(0, 1), (3, 2)]
    lhs = jnp.concatenate([saved, hfull], axis=0)
    row2 = jnp.where(d == 1, 2 * blk, 0)
    lhs2 = lax.dynamic_slice_in_dim(lhs, row2, 2 * blk, axis=1)
    rows = saved.shape[0]
    row3a = jnp.where(d == 1, 0, 3 * blk)
    row3b = jnp.where(d == 1, 0, blk)
    own = d * blk
    half = jnp.where(d == 1, blk, 0)
    edge = (d == 0) | (d == 3)
    pieces = []
    for c in range(chunks):
        sc = scaled[:, c * width:(c + 1) * width]
        srecv = lax.ppermute(sc, "dp", ends)
        rhs = jnp.concatenate([sc, srecv], axis=0)
        acc = lax.dot_general(
            lhs, rhs, (((0,), (0,)), ((), ())), preferred_element_type=jnp.float32
        )
        s2 = (
            lax.dot_general(lhs2[:rows], sc, (((0,), (0,)), ((), ())), preferred_element_type=jnp.float32)
            + lax.dot_general(lhs2[rows:], srecv, (((0,), (0,)), ((), ())), preferred_element_type=jnp.float32)
        ).astype(jnp.bfloat16)
        r2 = lax.ppermute(s2, "dp", [(1, 2), (2, 1)])
        s3 = (
            lax.dynamic_slice_in_dim(acc, row3a, blk, axis=0)
            + lax.dynamic_slice_in_dim(r2, row3b, blk, axis=0).astype(jnp.float32)
        ).astype(jnp.bfloat16)
        r3 = lax.ppermute(s3, "dp", [(1, 0), (2, 3)])
        extra = jnp.where(edge, r3, lax.dynamic_slice_in_dim(r2, half, blk, axis=0))
        pieces.append(
            lax.dynamic_slice_in_dim(acc, own, blk, axis=0) + extra.astype(jnp.float32)
        )
    return jnp.concatenate(pieces, axis=1), s2


def shards(grad_out, routes, gates, hidden, w_down):
    incoming = shifted(grad_out, "section", -1)[0]
    groups = lax.axis_size("expert")
    saved = hidden[0, 0, 0]
    weight = w_down[0, 0]
    slot_count = saved.shape[0]
    width = slot_count // groups
    model_width = incoming.shape[1]
    target = dispatch_targets(routes[0], groups, width)
    outgoing = dispatch_rows(incoming, gates[0], target, groups, width)
    line = lax.axis_size("dp") == 4 and saved.shape[1] % 4 == 0
    if line:
        hfull = send_hidden(saved)
    piece = lax.all_to_all(outgoing, "expert", split_axis=0, concat_axis=0, tiled=True)
    scaled = piece.reshape(slot_count, model_width)
    if line:
        weight_grad, anchor = line_weight_grad(saved, hfull, scaled, 4)
        late = scaled
    else:
        full = lax.dot_general(
            saved, scaled, (((0,), (0,)), ((), ())), preferred_element_type=jnp.float32
        )
        weight_grad = lax.psum_scatter(
            full.astype(jnp.bfloat16), "dp", scatter_dimension=0, tiled=True
        ).astype(jnp.float32)
        late = scaled
    grad_rows_out = jnp.einsum(
        "sd,hd->sh", late, weight, preferred_element_type=jnp.float32
    ).astype(jnp.bfloat16)
    grad_hidden = grad_rows_out.reshape(1, 1, 1, slot_count, saved.shape[1])
    return (grad_hidden, weight_grad.reshape(1, 1, weight_grad.shape[0], model_width))


def solution(mesh):
    placed = (
        P("section", ("dp", "expert"), None),
        P("section", ("dp", "expert"), None),
        P("section", ("dp", "expert"), None),
        P("section", "dp", "expert", None, None),
        P("section", "expert", None, None),
    )
    return jax.shard_map(
        shards,
        mesh=mesh,
        in_specs=placed,
        out_specs=(P("section", "dp", "expert", None, None), P("section", "expert", "dp", None)),
        check_vma=False,
    )
```

```python
import jax
import jax.numpy as jnp
from jax import lax
from jax.sharding import PartitionSpec as P


def shifted(value, axis, steps):
    count = lax.axis_size(axis)
    pairs = [(source, (source + steps) % count) for source in range(count)]
    return lax.ppermute(value, axis, pairs)


def dispatch_targets(ids, count, width):
    flat_ids = ids.reshape(-1)
    onehot = (flat_ids[:, None] == jnp.arange(count, dtype=jnp.int32)[None, :]).astype(jnp.int32)
    position = jnp.sum((jnp.cumsum(onehot, axis=0) - 1) * onehot, axis=1)
    return (flat_ids * width + position).reshape(ids.shape)


def dispatch_rows(rows, weights, target, count, width):
    slots = count * width
    total = None
    for k in range(target.shape[1]):
        scaled = (weights[:, k:k + 1] * rows.astype(jnp.float32)).astype(jnp.bfloat16)
        onehot = lax.broadcasted_iota(jnp.int32, (slots, rows.shape[0]), 0) == target[None, :, k]
        term = jnp.dot(onehot.astype(jnp.bfloat16), scaled, preferred_element_type=jnp.float32)
        total = term if total is None else total + term
    return total.astype(jnp.bfloat16).reshape(count, width, rows.shape[1])


def send_hidden(saved):
    d = lax.axis_index("dp")
    blk = saved.shape[1] // 4
    column_block = lax.broadcasted_iota(jnp.int32, saved.shape, 1) // blk
    hsend = jnp.where(column_block == d, jnp.zeros_like(saved), saved)
    return lax.ppermute(hsend, "dp", [(0, 1), (3, 2)])


def line_weight_grad(saved, hfull, scaled, chunks):
    d = lax.axis_index("dp")
    hid = saved.shape[1]
    blk = hid // 4
    width = scaled.shape[1] // chunks
    ends = [(0, 1), (3, 2)]
    lhs = jnp.concatenate([saved, hfull], axis=0)
    row2 = jnp.where(d == 1, 2 * blk, 0)
    lhs2 = lax.dynamic_slice_in_dim(lhs, row2, 2 * blk, axis=1)
    base = jnp.where(d <= 1, 0, 2 * blk)
    lhs_rest = lax.dynamic_slice_in_dim(lhs, base, 2 * blk, axis=1)
    row3a = jnp.where(d == 1, 0, 3 * blk) - base
    row3b = jnp.where(d == 1, 0, blk)
    own = d * blk - base
    half = jnp.where(d == 1, blk, 0)
    edge = (d == 0) | (d == 3)
    pieces = []
    for c in range(chunks):
        sc = scaled[:, c * width:(c + 1) * width]
        srecv = lax.ppermute(sc, "dp", ends)
        rhs = jnp.concatenate([sc, srecv], axis=0)
        acc = lax.dot_general(
            lhs_rest, rhs, (((0,), (0,)), ((), ())), preferred_element_type=jnp.float32
        )
        s2 = lax.dot_general(
            lhs2, rhs, (((0,), (0,)), ((), ())), preferred_element_type=jnp.float32
        ).astype(jnp.bfloat16)
        r2 = lax.ppermute(s2, "dp", [(1, 2), (2, 1)])
        s3 = (
            lax.dynamic_slice_in_dim(acc, row3a, blk, axis=0)
            + lax.dynamic_slice_in_dim(r2, row3b, blk, axis=0).astype(jnp.float32)
        ).astype(jnp.bfloat16)
        r3 = lax.ppermute(s3, "dp", [(1, 0), (2, 3)])
        extra = jnp.where(edge, r3, lax.dynamic_slice_in_dim(r2, half, blk, axis=0))
        pieces.append(
            lax.dynamic_slice_in_dim(acc, own, blk, axis=0) + extra.astype(jnp.float32)
        )
    return jnp.concatenate(pieces, axis=1), s2


def shards(grad_out, routes, gates, hidden, w_down):
    incoming = shifted(grad_out, "section", -1)[0]
    groups = lax.axis_size("expert")
    saved = hidden[0, 0, 0]
    weight = w_down[0, 0]
    slot_count = saved.shape[0]
    width = slot_count // groups
    model_width = incoming.shape[1]
    target = dispatch_targets(routes[0], groups, width)
    outgoing = dispatch_rows(incoming, gates[0], target, groups, width)
    line = lax.axis_size("dp") == 4 and saved.shape[1] % 4 == 0
    if line:
        hfull = send_hidden(saved)
    piece = lax.all_to_all(outgoing, "expert", split_axis=0, concat_axis=0, tiled=True)
    scaled = piece.reshape(slot_count, model_width)
    if line:
        weight_grad, anchor = line_weight_grad(saved, hfull, scaled, 4)
        late = scaled
    else:
        full = lax.dot_general(
            saved, scaled, (((0,), (0,)), ((), ())), preferred_element_type=jnp.float32
        )
        weight_grad = lax.psum_scatter(
            full.astype(jnp.bfloat16), "dp", scatter_dimension=0, tiled=True
        ).astype(jnp.float32)
        late = scaled
    grad_rows_out = jnp.einsum(
        "sd,hd->sh", late, weight, preferred_element_type=jnp.float32
    ).astype(jnp.bfloat16)
    grad_hidden = grad_rows_out.reshape(1, 1, 1, slot_count, saved.shape[1])
    return (grad_hidden, weight_grad.reshape(1, 1, weight_grad.shape[0], model_width))


def solution(mesh):
    placed = (
        P("section", ("dp", "expert"), None),
        P("section", ("dp", "expert"), None),
        P("section", ("dp", "expert"), None),
        P("section", "dp", "expert", None, None),
        P("section", "expert", None, None),
    )
    return jax.shard_map(
        shards,
        mesh=mesh,
        in_specs=placed,
        out_specs=(P("section", "dp", "expert", None, None), P("section", "expert", "dp", None)),
        check_vma=False,
    )
```
